512 devices in a mesh: gz: 64 (over x, z, y_lo), gx: 8 (over y_hi, core).
Axes of the slice: x: 4, y: 8 (y_hi: 4, y_lo: 2; y = y_hi * 2 + y_lo), z: 8, core: 2. Of those that a mesh axis runs over, the one named last changes fastest.
Arguments:
- latent: float32 [8, 128, 32, 128], P(None, 'gz', 'gx'), may hold values from -6 to 6
- condition: bfloat16 [8, 128, 32, 128], P(None, 'gz', 'gx'), may hold values from -6 to 6
- cotangent: float32 [8, 128, 32, 128], P(None, 'gz', 'gx'), may hold values from -6 to 6
- expand_kernel: bfloat16 [27, 64, 12], replicated, may hold values from -0.3125 to 0.3125
- mixing_matrix: bfloat16 [64, 64], replicated, may hold values from -0.75 to 0.75
- project_kernel: bfloat16 [27, 8, 64], replicated, may hold values from -0.15625 to 0.15625
- offsets: float32 [136], replicated, may hold values from -3 to 3
Outputs:
- restored: float32 [256, 64, 256], P('gz', 'gx')
- field_grad: float32 [256, 64, 256], P('gz', 'gx')
- condition_grad: float32 [8, 128, 32, 128], P(None, 'gz', 'gx')
- expand_grad: float32 [27, 64, 12], replicated
- mixing_grad: float32 [64, 64], replicated
- project_grad: float32 [27, 8, 64], replicated
- offset_grad: float32 [136], replicated
The draws below stay inside these ranges and needn't reach their ends.
All inputs are finite; a program needn't handle non-finite values.
Results may differ from the reference program's by a relative error of at most 0.007.
Values may be sent and summed in bfloat16 or wider, within the bound.
No kernel may reach another device: no remote copies, remote signals or barrier semaphores. Data moves between devices by JAX's collectives and lax.ppermute only.
A program may use at most 64 MiB of HBM per device.

```python
import jax
import jax.numpy as jnp
import numpy as np
from jax import lax

ZC = 2
XC = 4
YC = 128
H = 64
CH = 4
CC = 8
NZC = 128
NXC = 32


def steps_of(rng, shape, split, smallest, high):
    factor_of, own = 1.0, jax.random.fold_in(rng, 6)
    for position, shards_of in split:
        draws = jnp.exp(jax.random.uniform(jax.random.fold_in(own, position), (shards_of,), jnp.float32, smallest / len(split), high / len(split)))
        factor_of = factor_of * jnp.repeat(draws, shape[position] // shards_of).reshape([-1 if axis == position else 1 for axis in range(len(shape))])
    return factor_of


def gaussian(key, dims, scale, bound, split=(), kind=jnp.bfloat16):
    factor_of = steps_of(key, dims, split, -0.22, 0.18) if split else 1.0
    array = jax.random.normal(key, dims, jnp.float32) * scale * factor_of
    return jnp.minimum(jnp.maximum(array, -bound), bound).astype(kind)


def setup_inputs(seed: int = 0) -> dict:
    key_list = jax.random.split(jax.random.key(seed), 8)
    return {
        "latent": gaussian(key_list[0], (2 * CH, NZC, NXC, YC), 1.0, 6.0, ((1, 64), (2, 8)), jnp.float32),
        "condition": gaussian(key_list[1], (CC, NZC, NXC, YC), 1.0, 6.0, ((1, 64), (2, 8))),
        "cotangent": gaussian(key_list[2], (2 * CH, NZC, NXC, YC), 1.0, 6.0, ((1, 64), (2, 8)), jnp.float32),
        "expand_kernel": gaussian(key_list[3], (27, H, CH + CC), (27 * (CH + CC)) ** -0.5, 0.3125),
        "mixing_matrix": gaussian(key_list[4], (H, H), H ** -0.5, 0.75),
        "project_kernel": gaussian(key_list[5], (27, 2 * CH, H), (27 * H) ** -0.5, 0.15625),
        "offsets": gaussian(key_list[6], (2 * H + 2 * CH,), 0.5, 3.0, (), jnp.float32),
    }


def set_bits(value):
    parity_count = 0
    for bit_place in range(3):
        parity_count = parity_count + (value >> bit_place & 1)
    return parity_count

def haar_table():
    signs = np.zeros((8, 8), np.float32)
    for fine_index in range(8):
        for coef_index in range(8):
            parity = set_bits(fine_index & coef_index)
            signs[fine_index, coef_index] = (-1.0) ** parity / np.sqrt(8.0)
    return signs

def unsqueeze(coarse):
    haar_signs = jnp.asarray(haar_table())
    spread = jnp.einsum('pk,kzxy->pzxy', haar_signs, coarse, precision=lax.Precision.HIGHEST)
    planes, x_rows, y_cols = (coarse.shape[1], coarse.shape[2], coarse.shape[3])
    spread = spread.reshape(2, 2, 2, planes, x_rows, y_cols).transpose(3, 0, 4, 1, 5, 2)
    return spread.reshape(2 * planes, 2 * x_rows, 2 * y_cols)

def silu_slope(preact):
    sigma = jax.nn.sigmoid(preact)
    return sigma * (1.0 + preact * (1.0 - sigma))

def forward_taps(padded, weight, planes, x_rows):
    y_cols = padded.shape[3] - 2
    summed = None
    for tap_index in range(27):
        z_step, x_step, y_step = (tap_index // 9, tap_index // 3 % 3, tap_index % 3)
        sliced = padded[:, z_step:z_step + planes, x_step:x_step + x_rows, y_step:y_step + y_cols]
        product = jnp.einsum('oc,czxy->ozxy', weight[tap_index].astype(jnp.float32), sliced.astype(jnp.float32))
        summed = product if summed is None else summed + product
    return summed

def backward_taps(padded, weight, planes, x_rows):
    y_cols = padded.shape[3] - 2
    summed = None
    for tap_index in range(27):
        z_step, x_step, y_step = (tap_index // 9, tap_index // 3 % 3, tap_index % 3)
        sliced = padded[:, 2 - z_step:2 - z_step + planes, 2 - x_step:2 - x_step + x_rows, 2 - y_step:2 - y_step + y_cols]
        product = jnp.einsum('oc,ozxy->czxy', weight[tap_index].astype(jnp.float32), sliced.astype(jnp.float32))
        summed = product if summed is None else summed + product
    return summed

def weight_taps(grad, padded):
    planes, x_rows, y_cols = (grad.shape[1], grad.shape[2], grad.shape[3])
    result = []
    for tap_index in range(27):
        z_step, x_step, y_step = (tap_index // 9, tap_index // 3 % 3, tap_index % 3)
        sliced = padded[:, z_step:z_step + planes, x_step:x_step + x_rows, y_step:y_step + y_cols]
        result.append(jnp.einsum('ozxy,czxy->oc', grad.astype(jnp.float32), sliced.astype(jnp.float32)))
    return jnp.stack(result)

def frame_cols(tensor):
    return jnp.pad(tensor, ((0, 0), (0, 0), (1, 1), (1, 1)))

def reference(latent, condition, cotangent, expand_kernel, mixing_matrix, project_kernel, offsets):
    upper_half, lower_half = (latent[:CH], latent[CH:])
    cot_upper, cot_lower = (cotangent[:CH], cotangent[CH:])
    inputs = jnp.concatenate([upper_half.astype(jnp.bfloat16), condition], axis=0)
    input_frame = jnp.pad(inputs, ((0, 0), (2, 2), (1, 1), (1, 1)))
    expand_offset = offsets[:H][:, None, None, None]
    mixing_offset = offsets[H:2 * H][:, None, None, None]
    project_offset = offsets[2 * H:][:, None, None, None]
    block_total = NZC // ZC

    def hidden_block(first_plane):
        window = lax.dynamic_slice_in_dim(input_frame, first_plane, ZC + 4, 1)
        pre_one = forward_taps(window, expand_kernel, ZC + 2, NXC) + expand_offset
        act_one = jax.nn.silu(pre_one).astype(jnp.bfloat16)
        pre_two = jnp.einsum('oc,czxy->ozxy', mixing_matrix.astype(jnp.float32), act_one.astype(jnp.float32)) + mixing_offset
        planes = first_plane - 1 + jnp.arange(ZC + 2, dtype=jnp.int32)
        inside = ((planes >= 0) & (planes < NZC)).astype(jnp.float32)[None, :, None, None]
        act_two = (jax.nn.silu(pre_two) * inside).astype(jnp.bfloat16)
        return (window, pre_one, act_one, pre_two, act_two, inside)

    def score_block(block_index):
        first_plane = (block_index * ZC).astype(jnp.int32)
        window, pre_one, act_one, pre_two, act_two, inside = hidden_block(first_plane)
        return forward_taps(frame_cols(act_two), project_kernel, ZC, NXC) + project_offset
    scores = lax.map(score_block, jnp.arange(block_total, dtype=jnp.int32))
    scores = jnp.moveaxis(scores, 0, 1).reshape(2 * CH, NZC, NXC, YC)
    log_scale = jnp.tanh(scores[:CH])
    translate = scores[CH:]
    centered = lower_half - translate
    recovered = centered * jnp.exp(-log_scale)
    restored = unsqueeze(jnp.concatenate([upper_half, recovered], axis=0))
    score_grad = jnp.concatenate([cot_lower * centered * (1.0 - log_scale * log_scale), cot_lower], axis=0).astype(jnp.bfloat16)
    lower_grad = cot_lower * jnp.exp(log_scale)
    grad_frame = jnp.pad(score_grad, ((0, 0), (2, 2), (1, 1), (1, 1)))

    def grad_block(carry, block_index):
        first_plane = (block_index * ZC).astype(jnp.int32)
        window, pre_one, act_one, pre_two, act_two, inside = hidden_block(first_plane)
        act_frame = frame_cols(act_two)
        grad_window = lax.dynamic_slice_in_dim(grad_frame, first_plane, ZC + 4, 1)
        hidden_grad = backward_taps(grad_window, project_kernel, ZC + 2, NXC)
        mix_grad = (hidden_grad * silu_slope(pre_two)).astype(jnp.bfloat16)
        back_one = jnp.einsum('oc,ozxy->czxy', mixing_matrix.astype(jnp.float32), mix_grad.astype(jnp.float32))
        first_grad = (back_one * silu_slope(pre_one) * inside).astype(jnp.bfloat16)
        block_input = backward_taps(frame_cols(first_grad), expand_kernel, ZC, NXC)
        local_score = grad_window[:, 2:2 + ZC, 1:-1, 1:-1]
        inner_first = first_grad[:, 1:-1]
        inner_mix = mix_grad[:, 1:-1]
        updates = (weight_taps(inner_first, window[:, 1:-1]), jnp.einsum('ozxy,czxy->oc', inner_mix.astype(jnp.float32), act_one[:, 1:-1].astype(jnp.float32)), weight_taps(local_score, act_frame), jnp.concatenate([lax.optimization_barrier(jnp.sum(inner_first.astype(jnp.float32), axis=(1, 2, 3))), lax.optimization_barrier(jnp.sum(inner_mix.astype(jnp.float32), axis=(1, 2, 3))), lax.optimization_barrier(jnp.sum(local_score.astype(jnp.float32), axis=(1, 2, 3)))]))
        return (tuple((old + new for old, new in zip(carry, updates))), block_input)
    start = (jnp.zeros((27, H, CH + CC), jnp.float32), jnp.zeros((H, H), jnp.float32), jnp.zeros((27, 2 * CH, H), jnp.float32), jnp.zeros((2 * H + 2 * CH,), jnp.float32))
    sums, input_grad = lax.scan(grad_block, start, jnp.arange(block_total, dtype=jnp.int32))
    input_grad = jnp.moveaxis(input_grad, 0, 1).reshape(CH + CC, NZC, NXC, YC)
    field_grad = unsqueeze(jnp.concatenate([cot_upper + input_grad[:CH], lower_grad], axis=0))
    condition_grad = input_grad[CH:]
    factor = 1.0 / np.sqrt(float(ZC * XC * YC))
    return (restored, field_grad, condition_grad, sums[0] * factor, sums[1] * factor, sums[2] * factor, sums[3] * factor)
```

```python
import math

import jax
import jax.numpy as jnp
import numpy as np
from jax import lax
from jax.sharding import PartitionSpec as P

CH = 4


def extended(cells, sides, width):
    for axis, dim in sides:
        count = lax.axis_size(axis)
        ends = count - 1
        head = lax.slice_in_dim(cells, 0, width, axis=dim)
        tail = lax.slice_in_dim(cells, cells.shape[dim] - width, cells.shape[dim], axis=dim)
        cells = jnp.concatenate(
            [
                lax.ppermute(tail, axis, [(i, (i + 1) % count) for i in range(ends)]),
                cells,
                lax.ppermute(head, axis, [((i + 1) % count, i) for i in range(ends)]),
            ],
            axis=dim,
        )
    return cells


def set_bits(value):
    parity_count = 0
    for bit_place in range(3):
        parity_count = parity_count + (value >> bit_place & 1)
    return parity_count


def haar_table():
    signs = np.zeros((8, 8), np.float32)
    for fine_index in range(8):
        for coef_index in range(8):
            parity = set_bits(fine_index & coef_index)
            signs[fine_index, coef_index] = (-1.0) ** parity / np.sqrt(8.0)
    return signs


def unsqueeze(coarse):
    haar_signs = jnp.asarray(haar_table())
    spread = jnp.einsum("pk,kzxy->pzxy", haar_signs, coarse, precision=lax.Precision.HIGHEST)
    planes, x_rows, y_cols = (coarse.shape[1], coarse.shape[2], coarse.shape[3])
    spread = spread.reshape(2, 2, 2, planes, x_rows, y_cols).transpose(3, 0, 4, 1, 5, 2)
    return spread.reshape(2 * planes, 2 * x_rows, 2 * y_cols)


def silu_slope(preact):
    sigma = jax.nn.sigmoid(preact)
    return sigma * (1.0 + preact * (1.0 - sigma))


def forward_taps(padded, weight, planes, x_rows):
    y_cols = padded.shape[3] - 2
    summed = None
    for tap_index in range(27):
        z_step, x_step, y_step = (tap_index // 9, tap_index // 3 % 3, tap_index % 3)
        sliced = padded[
            :, z_step : z_step + planes, x_step : x_step + x_rows, y_step : y_step + y_cols
        ]
        product = jnp.einsum(
            "oc,czxy->ozxy", weight[tap_index], sliced, preferred_element_type=jnp.float32
        )
        summed = product if summed is None else summed + product
    return summed


def backward_taps(padded, weight, planes, x_rows):
    y_cols = padded.shape[3] - 2
    summed = None
    for tap_index in range(27):
        z_step, x_step, y_step = (tap_index // 9, tap_index // 3 % 3, tap_index % 3)
        sliced = padded[
            :,
            2 - z_step : 2 - z_step + planes,
            2 - x_step : 2 - x_step + x_rows,
            2 - y_step : 2 - y_step + y_cols,
        ]
        product = jnp.einsum(
            "oc,ozxy->czxy", weight[tap_index], sliced, preferred_element_type=jnp.float32
        )
        summed = product if summed is None else summed + product
    return summed


def weight_taps(grad, padded):
    planes, x_rows, y_cols = (grad.shape[1], grad.shape[2], grad.shape[3])
    result = []
    for tap_index in range(27):
        z_step, x_step, y_step = (tap_index // 9, tap_index // 3 % 3, tap_index % 3)
        sliced = padded[
            :, z_step : z_step + planes, x_step : x_step + x_rows, y_step : y_step + y_cols
        ]
        result.append(jnp.einsum("ozxy,czxy->oc", grad, sliced, preferred_element_type=jnp.float32))
    return jnp.stack(result)


def frame_cols(tensor):
    return jnp.pad(tensor, ((0, 0), (0, 0), (0, 0), (1, 1)))


def channel_sums(tensor):
    return jnp.sum(tensor.astype(jnp.float32), axis=(1, 2, 3))


def butterfly_sum(flat, axes):
    for axis in axes:
        count = lax.axis_size(axis)
        if count & (count - 1):
            flat = lax.psum(flat, axis)
            continue
        bit = 1
        while bit < count:
            flat = flat + lax.ppermute(flat, axis, [(i, i ^ bit) for i in range(count)])
            bit *= 2
    return flat


def per_device(latent, condition, cotangent, expand_kernel, mixing_matrix, project_kernel, offsets):
    planes, x_rows, y_cols = (latent.shape[1], latent.shape[2], latent.shape[3])
    hidden_width = mixing_matrix.shape[0]
    upper_half, lower_half = (latent[:CH], latent[CH:])
    cot_upper, cot_lower = (cotangent[:CH], cotangent[CH:])
    expand_offset = offsets[:hidden_width][:, None, None, None]
    mixing_offset = offsets[hidden_width : 2 * hidden_width][:, None, None, None]
    project_offset = offsets[2 * hidden_width :][:, None, None, None]
    inputs = jnp.concatenate([upper_half.astype(jnp.bfloat16), condition], axis=0)
    framed = frame_cols(extended(inputs, (("gz", 1), ("gx", 2)), 1))
    pre_one = forward_taps(framed, expand_kernel, planes, x_rows) + expand_offset
    act_one = jax.nn.silu(pre_one).astype(jnp.bfloat16)
    pre_two = (
        jnp.einsum("oc,czxy->ozxy", mixing_matrix, act_one, preferred_element_type=jnp.float32)
        + mixing_offset
    )
    act_two = jax.nn.silu(pre_two).astype(jnp.bfloat16)
    act_frame = frame_cols(extended(act_two, (("gz", 1), ("gx", 2)), 1))
    scores = forward_taps(act_frame, project_kernel, planes, x_rows) + project_offset
    log_scale = jnp.tanh(scores[:CH])
    centered = lower_half - scores[CH:]
    recovered = centered * jnp.exp(-log_scale)
    score_grad = jnp.concatenate(
        [cot_lower * centered * (1.0 - log_scale * log_scale), cot_lower], axis=0
    ).astype(jnp.bfloat16)
    recovered, score_grad, lower_grad = (recovered, score_grad, cot_lower * jnp.exp(log_scale))
    score_frame = frame_cols(extended(score_grad, (("gz", 1), ("gx", 2)), 1))
    hidden_grad = backward_taps(score_frame, project_kernel, planes, x_rows)
    mix_grad = (hidden_grad * silu_slope(pre_two)).astype(jnp.bfloat16)
    back_one = jnp.einsum(
        "oc,ozxy->czxy", mixing_matrix, mix_grad, preferred_element_type=jnp.float32
    )
    first_grad = (back_one * silu_slope(pre_one)).astype(jnp.bfloat16)
    first_frame = frame_cols(extended(first_grad, (("gz", 1), ("gx", 2)), 1))
    input_grad = backward_taps(first_frame, expand_kernel, planes, x_rows)
    inner_first, inner_mix, inner_act = (first_grad, mix_grad, act_one)
    expand_term = weight_taps(inner_first, framed)
    mixing_term = jnp.einsum(
        "ozxy,czxy->oc", inner_mix, inner_act, preferred_element_type=jnp.float32
    )
    project_term = weight_taps(score_grad, act_frame)
    offset_term = jnp.concatenate(
        [channel_sums(inner_first), channel_sums(inner_mix), channel_sums(score_grad)]
    )
    terms = (expand_term, mixing_term, project_term, offset_term)
    flat = butterfly_sum(jnp.concatenate([t.reshape(-1) for t in terms]), ("gx", "gz"))
    pieces, start = [], 0
    for t in terms:
        pieces.append(flat[start : start + t.size].reshape(t.shape))
        start += t.size
    expand_sum, mixing_sum, project_sum, offset_sum = pieces
    restored = unsqueeze(jnp.concatenate([upper_half, recovered], axis=0))
    field_grad = unsqueeze(jnp.concatenate([cot_upper + input_grad[:CH], lower_grad], axis=0))
    condition_grad = input_grad[CH:]
    factor = 1.0 / math.sqrt(float(planes * x_rows * y_cols))
    return (
        restored,
        field_grad,
        condition_grad,
        expand_sum * factor,
        mixing_sum * factor,
        project_sum * factor,
        offset_sum * factor,
    )


def solution(mesh):
    placed = (
        P(None, "gz", "gx", None),
        P(None, "gz", "gx", None),
        P(None, "gz", "gx", None),
        P(),
        P(),
        P(),
        P(),
    )
    return jax.shard_map(
        per_device,
        mesh=mesh,
        in_specs=placed,
        out_specs=(
            P("gz", "gx", None),
            P("gz", "gx", None),
            P(None, "gz", "gx", None),
            P(),
            P(),
            P(),
            P(),
        ),
        check_vma=False,
    )
```

```python
import math

import jax
import jax.numpy as jnp
import numpy as np
from jax import lax
from jax.sharding import PartitionSpec as P

CH = 4


def extended(cells, sides, width):
    for axis, dim in sides:
        count = lax.axis_size(axis)
        ends = count - 1
        head = lax.slice_in_dim(cells, 0, width, axis=dim)
        tail = lax.slice_in_dim(cells, cells.shape[dim] - width, cells.shape[dim], axis=dim)
        cells = jnp.concatenate(
            [
                lax.ppermute(tail, axis, [(i, (i + 1) % count) for i in range(ends)]),
                cells,
                lax.ppermute(head, axis, [((i + 1) % count, i) for i in range(ends)]),
            ],
            axis=dim,
        )
    return cells


def set_bits(value):
    parity_count = 0
    for bit_place in range(3):
        parity_count = parity_count + (value >> bit_place & 1)
    return parity_count


def haar_table():
    signs = np.zeros((8, 8), np.float32)
    for fine_index in range(8):
        for coef_index in range(8):
            parity = set_bits(fine_index & coef_index)
            signs[fine_index, coef_index] = (-1.0) ** parity / np.sqrt(8.0)
    return signs


def unsqueeze(coarse):
    haar_signs = jnp.asarray(haar_table())
    spread = jnp.einsum("pk,kzxy->pzxy", haar_signs, coarse, precision=lax.Precision.HIGHEST)
    planes, x_rows, y_cols = (coarse.shape[1], coarse.shape[2], coarse.shape[3])
    spread = spread.reshape(2, 2, 2, planes, x_rows, y_cols).transpose(3, 0, 4, 1, 5, 2)
    return spread.reshape(2 * planes, 2 * x_rows, 2 * y_cols)


def silu_slope(preact):
    sigma = jax.nn.sigmoid(preact)
    return sigma * (1.0 + preact * (1.0 - sigma))


def forward_taps(padded, weight, planes, x_rows):
    y_cols = padded.shape[3] - 2
    summed = None
    for tap_index in range(27):
        z_step, x_step, y_step = (tap_index // 9, tap_index // 3 % 3, tap_index % 3)
        sliced = padded[
            :, z_step : z_step + planes, x_step : x_step + x_rows, y_step : y_step + y_cols
        ]
        product = jnp.einsum(
            "oc,czxy->ozxy", weight[tap_index], sliced, preferred_element_type=jnp.float32
        )
        summed = product if summed is None else summed + product
    return summed


def backward_taps(padded, weight, planes, x_rows):
    y_cols = padded.shape[3] - 2
    summed = None
    for tap_index in range(27):
        z_step, x_step, y_step = (tap_index // 9, tap_index // 3 % 3, tap_index % 3)
        sliced = padded[
            :,
            2 - z_step : 2 - z_step + planes,
            2 - x_step : 2 - x_step + x_rows,
            2 - y_step : 2 - y_step + y_cols,
        ]
        product = jnp.einsum(
            "oc,ozxy->czxy", weight[tap_index], sliced, preferred_element_type=jnp.float32
        )
        summed = product if summed is None else summed + product
    return summed


def weight_taps(grad, padded):
    planes, x_rows, y_cols = (grad.shape[1], grad.shape[2], grad.shape[3])
    result = []
    for tap_index in range(27):
        z_step, x_step, y_step = (tap_index // 9, tap_index // 3 % 3, tap_index % 3)
        sliced = padded[
            :, z_step : z_step + planes, x_step : x_step + x_rows, y_step : y_step + y_cols
        ]
        result.append(jnp.einsum("ozxy,czxy->oc", grad, sliced, preferred_element_type=jnp.float32))
    return jnp.stack(result)


def frame_cols(tensor):
    return jnp.pad(tensor, ((0, 0), (0, 0), (0, 0), (1, 1)))


def channel_sums(tensor):
    return jnp.sum(tensor.astype(jnp.float32), axis=(1, 2, 3))


def butterfly_sum(flat, axes):
    for axis in axes:
        count = lax.axis_size(axis)
        if count & (count - 1):
            flat = lax.psum(flat, axis)
            continue
        bit = 1
        while bit < count:
            flat = flat + lax.ppermute(flat, axis, [(i, i ^ bit) for i in range(count)])
            bit *= 2
    return flat


def replicated_sum(flat, scatter_axis, other_axes):
    total = flat.shape[0]
    count = lax.axis_size(scatter_axis)
    chunks = jnp.pad(flat, (0, (-total) % count)).reshape(count, -1)
    owned = lax.all_to_all(chunks, scatter_axis, 0, 0, tiled=False).sum(0)
    owned = butterfly_sum(owned, other_axes)
    spread = lax.all_to_all(jnp.broadcast_to(owned, (count,) + owned.shape), scatter_axis, 0, 0, tiled=False)
    return spread.reshape(-1)[:total]


def per_device(latent, condition, cotangent, expand_kernel, mixing_matrix, project_kernel, offsets):
    planes, x_rows, y_cols = (latent.shape[1], latent.shape[2], latent.shape[3])
    hidden_width = mixing_matrix.shape[0]
    upper_half, lower_half = (latent[:CH], latent[CH:])
    cot_upper, cot_lower = (cotangent[:CH], cotangent[CH:])
    expand_offset = offsets[:hidden_width][:, None, None, None]
    mixing_offset = offsets[hidden_width : 2 * hidden_width][:, None, None, None]
    project_offset = offsets[2 * hidden_width :][:, None, None, None]
    inputs = jnp.concatenate([upper_half.astype(jnp.bfloat16), condition], axis=0)
    framed = frame_cols(extended(inputs, (("gz", 1), ("gx", 2)), 1))
    pre_one = forward_taps(framed, expand_kernel, planes, x_rows) + expand_offset
    act_one = jax.nn.silu(pre_one).astype(jnp.bfloat16)
    pre_two = (
        jnp.einsum("oc,czxy->ozxy", mixing_matrix, act_one, preferred_element_type=jnp.float32)
        + mixing_offset
    )
    act_two = jax.nn.silu(pre_two).astype(jnp.bfloat16)
    act_frame = frame_cols(extended(act_two, (("gz", 1), ("gx", 2)), 1))
    scores = forward_taps(act_frame, project_kernel, planes, x_rows) + project_offset
    log_scale = jnp.tanh(scores[:CH])
    centered = lower_half - scores[CH:]
    recovered = centered * jnp.exp(-log_scale)
    score_grad = jnp.concatenate(
        [cot_lower * centered * (1.0 - log_scale * log_scale), cot_lower], axis=0
    ).astype(jnp.bfloat16)
    recovered, score_grad, lower_grad = (recovered, score_grad, cot_lower * jnp.exp(log_scale))
    score_frame = frame_cols(extended(score_grad, (("gz", 1), ("gx", 2)), 1))
    hidden_grad = backward_taps(score_frame, project_kernel, planes, x_rows)
    mix_grad = (hidden_grad * silu_slope(pre_two)).astype(jnp.bfloat16)
    back_one = jnp.einsum(
        "oc,ozxy->czxy", mixing_matrix, mix_grad, preferred_element_type=jnp.float32
    )
    first_grad = (back_one * silu_slope(pre_one)).astype(jnp.bfloat16)
    first_frame = frame_cols(extended(first_grad, (("gz", 1), ("gx", 2)), 1))
    input_grad = backward_taps(first_frame, expand_kernel, planes, x_rows)
    inner_first, inner_mix, inner_act = (first_grad, mix_grad, act_one)
    expand_term = weight_taps(inner_first, framed)
    mixing_term = jnp.einsum(
        "ozxy,czxy->oc", inner_mix, inner_act, preferred_element_type=jnp.float32
    )
    project_term = weight_taps(score_grad, act_frame)
    offset_term = jnp.concatenate(
        [channel_sums(inner_first), channel_sums(inner_mix), channel_sums(score_grad)]
    )
    terms = (expand_term, mixing_term, project_term, offset_term)
    flat = replicated_sum(jnp.concatenate([t.reshape(-1) for t in terms]), "gz", ("gx",))
    pieces, start = [], 0
    for t in terms:
        pieces.append(flat[start : start + t.size].reshape(t.shape))
        start += t.size
    expand_sum, mixing_sum, project_sum, offset_sum = pieces
    restored = unsqueeze(jnp.concatenate([upper_half, recovered], axis=0))
    field_grad = unsqueeze(jnp.concatenate([cot_upper + input_grad[:CH], lower_grad], axis=0))
    condition_grad = input_grad[CH:]
    factor = 1.0 / math.sqrt(float(planes * x_rows * y_cols))
    return (
        restored,
        field_grad,
        condition_grad,
        expand_sum * factor,
        mixing_sum * factor,
        project_sum * factor,
        offset_sum * factor,
    )


def solution(mesh):
    placed = (
        P(None, "gz", "gx", None),
        P(None, "gz", "gx", None),
        P(None, "gz", "gx", None),
        P(),
        P(),
        P(),
        P(),
    )
    return jax.shard_map(
        per_device,
        mesh=mesh,
        in_specs=placed,
        out_specs=(
            P("gz", "gx", None),
            P("gz", "gx", None),
            P(None, "gz", "gx", None),
            P(),
            P(),
            P(),
            P(),
        ),
        check_vma=False,
    )
```

```python
import math

import jax
import jax.numpy as jnp
import numpy as np
from jax import lax
from jax.sharding import PartitionSpec as P

CH = 4


def extended(cells, sides, width):
    for axis, dim in sides:
        count = lax.axis_size(axis)
        ends = count - 1
        head = lax.slice_in_dim(cells, 0, width, axis=dim)
        tail = lax.slice_in_dim(cells, cells.shape[dim] - width, cells.shape[dim], axis=dim)
        cells = jnp.concatenate(
            [
                lax.ppermute(tail, axis, [(i, (i + 1) % count) for i in range(ends)]),
                cells,
                lax.ppermute(head, axis, [((i + 1) % count, i) for i in range(ends)]),
            ],
            axis=dim,
        )
    return cells


def set_bits(value):
    parity_count = 0
    for bit_place in range(3):
        parity_count = parity_count + (value >> bit_place & 1)
    return parity_count


def haar_table():
    signs = np.zeros((8, 8), np.float32)
    for fine_index in range(8):
        for coef_index in range(8):
            parity = set_bits(fine_index & coef_index)
            signs[fine_index, coef_index] = (-1.0) ** parity / np.sqrt(8.0)
    return signs


def unsqueeze(coarse):
    haar_signs = jnp.asarray(haar_table())
    spread = jnp.einsum("pk,kzxy->pzxy", haar_signs, coarse, precision=lax.Precision.HIGHEST)
    planes, x_rows, y_cols = (coarse.shape[1], coarse.shape[2], coarse.shape[3])
    spread = spread.reshape(2, 2, 2, planes, x_rows, y_cols).transpose(3, 0, 4, 1, 5, 2)
    return spread.reshape(2 * planes, 2 * x_rows, 2 * y_cols)


def silu_slope(preact):
    sigma = jax.nn.sigmoid(preact)
    return sigma * (1.0 + preact * (1.0 - sigma))


def conv_kernel(weight):
    return weight.reshape((3, 3, 3) + weight.shape[1:])


def forward_taps(padded, weight, planes, x_rows):
    kernel = jnp.transpose(conv_kernel(weight), (3, 4, 0, 1, 2))
    out = lax.conv_general_dilated(
        padded[None], kernel, (1, 1, 1), "VALID",
        dimension_numbers=("NCDHW", "OIDHW", "NCDHW"), preferred_element_type=jnp.float32,
    )
    return out[0]


def backward_taps(padded, weight, planes, x_rows):
    kernel = jnp.transpose(conv_kernel(weight)[::-1, ::-1, ::-1], (4, 3, 0, 1, 2))
    out = lax.conv_general_dilated(
        padded[None], kernel, (1, 1, 1), "VALID",
        dimension_numbers=("NCDHW", "OIDHW", "NCDHW"), preferred_element_type=jnp.float32,
    )
    return out[0]


def weight_taps(grad, padded):
    out = lax.conv_general_dilated(
        padded[:, None], grad[:, None], (1, 1, 1), "VALID",
        dimension_numbers=("NCDHW", "OIDHW", "NCDHW"), preferred_element_type=jnp.float32,
    )
    taps = jnp.transpose(out, (2, 3, 4, 1, 0))
    return taps.reshape((27,) + taps.shape[3:])


def frame_cols(tensor):
    return jnp.pad(tensor, ((0, 0), (0, 0), (0, 0), (1, 1)))


def channel_sums(tensor):
    return jnp.sum(tensor.astype(jnp.float32), axis=(1, 2, 3))


def butterfly_sum(flat, axes):
    for axis in axes:
        count = lax.axis_size(axis)
        if count & (count - 1):
            flat = lax.psum(flat, axis)
            continue
        bit = 1
        while bit < count:
            flat = flat + lax.ppermute(flat, axis, [(i, i ^ bit) for i in range(count)])
            bit *= 2
    return flat


def replicated_sum(flat, scatter_axis, other_axes):
    total = flat.shape[0]
    count = lax.axis_size(scatter_axis)
    chunks = jnp.pad(flat, (0, (-total) % count)).reshape(count, -1)
    owned = lax.all_to_all(chunks, scatter_axis, 0, 0, tiled=False).sum(0)
    owned = butterfly_sum(owned, other_axes)
    spread = lax.all_to_all(jnp.broadcast_to(owned, (count,) + owned.shape), scatter_axis, 0, 0, tiled=False)
    return spread.reshape(-1)[:total]


def per_device(latent, condition, cotangent, expand_kernel, mixing_matrix, project_kernel, offsets):
    planes, x_rows, y_cols = (latent.shape[1], latent.shape[2], latent.shape[3])
    hidden_width = mixing_matrix.shape[0]
    upper_half, lower_half = (latent[:CH], latent[CH:])
    cot_upper, cot_lower = (cotangent[:CH], cotangent[CH:])
    expand_offset = offsets[:hidden_width][:, None, None, None]
    mixing_offset = offsets[hidden_width : 2 * hidden_width][:, None, None, None]
    project_offset = offsets[2 * hidden_width :][:, None, None, None]
    inputs = jnp.concatenate([upper_half.astype(jnp.bfloat16), condition], axis=0)
    framed = frame_cols(extended(inputs, (("gz", 1), ("gx", 2)), 1))
    pre_one = forward_taps(framed, expand_kernel, planes, x_rows) + expand_offset
    act_one = jax.nn.silu(pre_one).astype(jnp.bfloat16)
    pre_two = (
        jnp.einsum("oc,czxy->ozxy", mixing_matrix, act_one, preferred_element_type=jnp.float32)
        + mixing_offset
    )
    act_two = jax.nn.silu(pre_two).astype(jnp.bfloat16)
    act_frame = frame_cols(extended(act_two, (("gz", 1), ("gx", 2)), 1))
    scores = forward_taps(act_frame, project_kernel, planes, x_rows) + project_offset
    log_scale = jnp.tanh(scores[:CH])
    centered = lower_half - scores[CH:]
    recovered = centered * jnp.exp(-log_scale)
    score_grad = jnp.concatenate(
        [cot_lower * centered * (1.0 - log_scale * log_scale), cot_lower], axis=0
    ).astype(jnp.bfloat16)
    recovered, score_grad, lower_grad = (recovered, score_grad, cot_lower * jnp.exp(log_scale))
    score_frame = frame_cols(extended(score_grad, (("gz", 1), ("gx", 2)), 1))
    hidden_grad = backward_taps(score_frame, project_kernel, planes, x_rows)
    mix_grad = (hidden_grad * silu_slope(pre_two)).astype(jnp.bfloat16)
    back_one = jnp.einsum(
        "oc,ozxy->czxy", mixing_matrix, mix_grad, preferred_element_type=jnp.float32
    )
    first_grad = (back_one * silu_slope(pre_one)).astype(jnp.bfloat16)
    first_frame = frame_cols(extended(first_grad, (("gz", 1), ("gx", 2)), 1))
    input_grad = backward_taps(first_frame, expand_kernel, planes, x_rows)
    inner_first, inner_mix, inner_act = (first_grad, mix_grad, act_one)
    expand_term = weight_taps(inner_first, framed)
    mixing_term = jnp.einsum(
        "ozxy,czxy->oc", inner_mix, inner_act, preferred_element_type=jnp.float32
    )
    project_term = weight_taps(score_grad, act_frame)
    offset_term = jnp.concatenate(
        [channel_sums(inner_first), channel_sums(inner_mix), channel_sums(score_grad)]
    )
    terms = (expand_term, mixing_term, project_term, offset_term)
    flat = replicated_sum(jnp.concatenate([t.reshape(-1) for t in terms]), "gz", ("gx",))
    pieces, start = [], 0
    for t in terms:
        pieces.append(flat[start : start + t.size].reshape(t.shape))
        start += t.size
    expand_sum, mixing_sum, project_sum, offset_sum = pieces
    restored = unsqueeze(jnp.concatenate([upper_half, recovered], axis=0))
    field_grad = unsqueeze(jnp.concatenate([cot_upper + input_grad[:CH], lower_grad], axis=0))
    condition_grad = input_grad[CH:]
    factor = 1.0 / math.sqrt(float(planes * x_rows * y_cols))
    return (
        restored,
        field_grad,
        condition_grad,
        expand_sum * factor,
        mixing_sum * factor,
        project_sum * factor,
        offset_sum * factor,
    )


def solution(mesh):
    placed = (
        P(None, "gz", "gx", None),
        P(None, "gz", "gx", None),
        P(None, "gz", "gx", None),
        P(),
        P(),
        P(),
        P(),
    )
    return jax.shard_map(
        per_device,
        mesh=mesh,
        in_specs=placed,
        out_specs=(
            P("gz", "gx", None),
            P("gz", "gx", None),
            P(None, "gz", "gx", None),
            P(),
            P(),
            P(),
            P(),
        ),
        check_vma=False,
    )
```

```python
import math

import jax
import jax.numpy as jnp
import numpy as np
from jax import lax
from jax.sharding import PartitionSpec as P

CH = 4


def extended(cells, sides, width):
    for axis, dim in sides:
        count = lax.axis_size(axis)
        ends = count - 1
        head = lax.slice_in_dim(cells, 0, width, axis=dim)
        tail = lax.slice_in_dim(cells, cells.shape[dim] - width, cells.shape[dim], axis=dim)
        cells = jnp.concatenate(
            [
                lax.ppermute(tail, axis, [(i, (i + 1) % count) for i in range(ends)]),
                cells,
                lax.ppermute(head, axis, [((i + 1) % count, i) for i in range(ends)]),
            ],
            axis=dim,
        )
    return cells


def set_bits(value):
    parity_count = 0
    for bit_place in range(3):
        parity_count = parity_count + (value >> bit_place & 1)
    return parity_count


def haar_table():
    signs = np.zeros((8, 8), np.float32)
    for fine_index in range(8):
        for coef_index in range(8):
            parity = set_bits(fine_index & coef_index)
            signs[fine_index, coef_index] = (-1.0) ** parity / np.sqrt(8.0)
    return signs


def unsqueeze(coarse):
    haar_signs = jnp.asarray(haar_table())
    spread = jnp.einsum("pk,kzxy->pzxy", haar_signs, coarse, precision=lax.Precision.HIGHEST)
    planes, x_rows, y_cols = (coarse.shape[1], coarse.shape[2], coarse.shape[3])
    spread = spread.reshape(2, 2, 2, planes, x_rows, y_cols).transpose(3, 0, 4, 1, 5, 2)
    return spread.reshape(2 * planes, 2 * x_rows, 2 * y_cols)


def silu_slope(preact):
    sigma = jax.nn.sigmoid(preact)
    return sigma * (1.0 + preact * (1.0 - sigma))


def conv_kernel(weight):
    return weight.reshape((3, 3, 3) + weight.shape[1:])


def forward_taps(padded, weight, planes, x_rows):
    kernel = jnp.transpose(conv_kernel(weight), (3, 4, 0, 1, 2))
    out = lax.conv_general_dilated(
        padded[None], kernel, (1, 1, 1), "VALID",
        dimension_numbers=("NCDHW", "OIDHW", "NCDHW"), preferred_element_type=jnp.float32,
    )
    return out[0]


def backward_taps(padded, weight, planes, x_rows):
    kernel = jnp.transpose(conv_kernel(weight)[::-1, ::-1, ::-1], (4, 3, 0, 1, 2))
    out = lax.conv_general_dilated(
        padded[None], kernel, (1, 1, 1), "VALID",
        dimension_numbers=("NCDHW", "OIDHW", "NCDHW"), preferred_element_type=jnp.float32,
    )
    return out[0]


def weight_taps(grad, padded):
    planes, x_rows, y_cols = (grad.shape[1], grad.shape[2], grad.shape[3])
    result = []
    for tap_index in range(27):
        z_step, x_step, y_step = (tap_index // 9, tap_index // 3 % 3, tap_index % 3)
        sliced = padded[
            :, z_step : z_step + planes, x_step : x_step + x_rows, y_step : y_step + y_cols
        ]
        result.append(jnp.einsum("ozxy,czxy->oc", grad, sliced, preferred_element_type=jnp.float32))
    return jnp.stack(result)


def frame_cols(tensor):
    return jnp.pad(tensor, ((0, 0), (0, 0), (0, 0), (1, 1)))


def channel_sums(tensor):
    return jnp.sum(tensor.astype(jnp.float32), axis=(1, 2, 3))


def butterfly_sum(flat, axes):
    for axis in axes:
        count = lax.axis_size(axis)
        if count & (count - 1):
            flat = lax.psum(flat, axis)
            continue
        bit = 1
        while bit < count:
            flat = flat + lax.ppermute(flat, axis, [(i, i ^ bit) for i in range(count)])
            bit *= 2
    return flat


def replicated_sum(flat, scatter_axis, other_axes):
    total = flat.shape[0]
    count = lax.axis_size(scatter_axis)
    chunks = jnp.pad(flat, (0, (-total) % count)).reshape(count, -1)
    owned = lax.all_to_all(chunks, scatter_axis, 0, 0, tiled=False).sum(0)
    owned = butterfly_sum(owned, other_axes)
    spread = lax.all_to_all(jnp.broadcast_to(owned, (count,) + owned.shape), scatter_axis, 0, 0, tiled=False)
    return spread.reshape(-1)[:total]


def per_device(latent, condition, cotangent, expand_kernel, mixing_matrix, project_kernel, offsets):
    planes, x_rows, y_cols = (latent.shape[1], latent.shape[2], latent.shape[3])
    hidden_width = mixing_matrix.shape[0]
    upper_half, lower_half = (latent[:CH], latent[CH:])
    cot_upper, cot_lower = (cotangent[:CH], cotangent[CH:])
    expand_offset = offsets[:hidden_width][:, None, None, None]
    mixing_offset = offsets[hidden_width : 2 * hidden_width][:, None, None, None]
    project_offset = offsets[2 * hidden_width :][:, None, None, None]
    inputs = jnp.concatenate([upper_half.astype(jnp.bfloat16), condition], axis=0)
    framed = frame_cols(extended(inputs, (("gz", 1), ("gx", 2)), 1))
    pre_one = forward_taps(framed, expand_kernel, planes, x_rows) + expand_offset
    act_one = jax.nn.silu(pre_one).astype(jnp.bfloat16)
    pre_two = (
        jnp.einsum("oc,czxy->ozxy", mixing_matrix, act_one, preferred_element_type=jnp.float32)
        + mixing_offset
    )
    act_two = jax.nn.silu(pre_two).astype(jnp.bfloat16)
    act_frame = frame_cols(extended(act_two, (("gz", 1), ("gx", 2)), 1))
    scores = forward_taps(act_frame, project_kernel, planes, x_rows) + project_offset
    log_scale = jnp.tanh(scores[:CH])
    centered = lower_half - scores[CH:]
    recovered = centered * jnp.exp(-log_scale)
    score_grad = jnp.concatenate(
        [cot_lower * centered * (1.0 - log_scale * log_scale), cot_lower], axis=0
    ).astype(jnp.bfloat16)
    recovered, score_grad, lower_grad = (recovered, score_grad, cot_lower * jnp.exp(log_scale))
    score_frame = frame_cols(extended(score_grad, (("gz", 1), ("gx", 2)), 1))
    hidden_grad = backward_taps(score_frame, project_kernel, planes, x_rows)
    mix_grad = (hidden_grad * silu_slope(pre_two)).astype(jnp.bfloat16)
    back_one = jnp.einsum(
        "oc,ozxy->czxy", mixing_matrix, mix_grad, preferred_element_type=jnp.float32
    )
    first_grad = (back_one * silu_slope(pre_one)).astype(jnp.bfloat16)
    first_frame = frame_cols(extended(first_grad, (("gz", 1), ("gx", 2)), 1))
    input_grad = backward_taps(first_frame, expand_kernel, planes, x_rows)
    inner_first, inner_mix, inner_act = (first_grad, mix_grad, act_one)
    expand_term = weight_taps(inner_first, framed)
    mixing_term = jnp.einsum(
        "ozxy,czxy->oc", inner_mix, inner_act, preferred_element_type=jnp.float32
    )
    project_term = weight_taps(score_grad, act_frame)
    offset_term = jnp.concatenate(
        [channel_sums(inner_first), channel_sums(inner_mix), channel_sums(score_grad)]
    )
    terms = (expand_term, mixing_term, project_term, offset_term)
    flat = replicated_sum(jnp.concatenate([t.reshape(-1) for t in terms]), "gz", ("gx",))
    pieces, start = [], 0
    for t in terms:
        pieces.append(flat[start : start + t.size].reshape(t.shape))
        start += t.size
    expand_sum, mixing_sum, project_sum, offset_sum = pieces
    restored = unsqueeze(jnp.concatenate([upper_half, recovered], axis=0))
    field_grad = unsqueeze(jnp.concatenate([cot_upper + input_grad[:CH], lower_grad], axis=0))
    condition_grad = input_grad[CH:]
    factor = 1.0 / math.sqrt(float(planes * x_rows * y_cols))
    return (
        restored,
        field_grad,
        condition_grad,
        expand_sum * factor,
        mixing_sum * factor,
        project_sum * factor,
        offset_sum * factor,
    )


def solution(mesh):
    placed = (
        P(None, "gz", "gx", None),
        P(None, "gz", "gx", None),
        P(None, "gz", "gx", None),
        P(),
        P(),
        P(),
        P(),
    )
    return jax.shard_map(
        per_device,
        mesh=mesh,
        in_specs=placed,
        out_specs=(
            P("gz", "gx", None),
            P("gz", "gx", None),
            P(None, "gz", "gx", None),
            P(),
            P(),
            P(),
            P(),
        ),
        check_vma=False,
    )
```

```python
import math

import jax
import jax.numpy as jnp
import numpy as np
from jax import lax
from jax.sharding import PartitionSpec as P

CH = 4


def extended(cells, sides, width):
    for axis, dim in sides:
        count = lax.axis_size(axis)
        ends = count - 1
        head = lax.slice_in_dim(cells, 0, width, axis=dim)
        tail = lax.slice_in_dim(cells, cells.shape[dim] - width, cells.shape[dim], axis=dim)
        cells = jnp.concatenate(
            [
                lax.ppermute(tail, axis, [(i, (i + 1) % count) for i in range(ends)]),
                cells,
                lax.ppermute(head, axis, [((i + 1) % count, i) for i in range(ends)]),
            ],
            axis=dim,
        )
    return cells


def set_bits(value):
    parity_count = 0
    for bit_place in range(3):
        parity_count = parity_count + (value >> bit_place & 1)
    return parity_count


def haar_table():
    signs = np.zeros((8, 8), np.float32)
    for fine_index in range(8):
        for coef_index in range(8):
            parity = set_bits(fine_index & coef_index)
            signs[fine_index, coef_index] = (-1.0) ** parity / np.sqrt(8.0)
    return signs


def unsqueeze(coarse):
    haar_signs = jnp.asarray(haar_table())
    spread = jnp.einsum("pk,kzxy->pzxy", haar_signs, coarse, precision=lax.Precision.HIGHEST)
    planes, x_rows, y_cols = (coarse.shape[1], coarse.shape[2], coarse.shape[3])
    spread = spread.reshape(2, 2, 2, planes, x_rows, y_cols).transpose(3, 0, 4, 1, 5, 2)
    return spread.reshape(2 * planes, 2 * x_rows, 2 * y_cols)


def silu_slope(preact):
    sigma = jax.nn.sigmoid(preact)
    return sigma * (1.0 + preact * (1.0 - sigma))


def forward_taps(padded, weight, planes, x_rows):
    y_cols = padded.shape[3] - 2
    summed = None
    for tap_index in range(27):
        z_step, x_step, y_step = (tap_index // 9, tap_index // 3 % 3, tap_index % 3)
        sliced = padded[
            :, z_step : z_step + planes, x_step : x_step + x_rows, y_step : y_step + y_cols
        ]
        product = jnp.einsum(
            "oc,czxy->ozxy", weight[tap_index], sliced, preferred_element_type=jnp.float32
        )
        summed = product if summed is None else summed + product
    return summed


def backward_taps(padded, weight, planes, x_rows):
    y_cols = padded.shape[3] - 2
    summed = None
    for tap_index in range(27):
        z_step, x_step, y_step = (tap_index // 9, tap_index // 3 % 3, tap_index % 3)
        sliced = padded[
            :,
            2 - z_step : 2 - z_step + planes,
            2 - x_step : 2 - x_step + x_rows,
            2 - y_step : 2 - y_step + y_cols,
        ]
        product = jnp.einsum(
            "oc,ozxy->czxy", weight[tap_index], sliced, preferred_element_type=jnp.float32
        )
        summed = product if summed is None else summed + product
    return summed


def weight_taps(grad, padded):
    planes, x_rows, y_cols = (grad.shape[1], grad.shape[2], grad.shape[3])
    result = []
    for tap_index in range(27):
        z_step, x_step, y_step = (tap_index // 9, tap_index // 3 % 3, tap_index % 3)
        sliced = padded[
            :, z_step : z_step + planes, x_step : x_step + x_rows, y_step : y_step + y_cols
        ]
        result.append(jnp.einsum("ozxy,czxy->oc", grad, sliced, preferred_element_type=jnp.float32))
    return jnp.stack(result)


def frame_cols(tensor):
    return jnp.pad(tensor, ((0, 0), (0, 0), (0, 0), (1, 1)))


def channel_sums(tensor):
    return jnp.sum(tensor.astype(jnp.float32), axis=(1, 2, 3))


def butterfly_sum(flat, axes):
    for axis in axes:
        count = lax.axis_size(axis)
        if count & (count - 1):
            flat = lax.psum(flat, axis)
            continue
        bit = 1
        while bit < count:
            flat = flat + lax.ppermute(flat, axis, [(i, i ^ bit) for i in range(count)])
            bit *= 2
    return flat


def replicated_sum(flat, scatter_axis, other_axes):
    total = flat.shape[0]
    count = lax.axis_size(scatter_axis)
    chunks = jnp.pad(flat, (0, (-total) % count)).reshape(count, -1)
    owned = lax.all_to_all(chunks, scatter_axis, 0, 0, tiled=False).sum(0)
    owned = butterfly_sum(owned, other_axes)
    spread = lax.all_to_all(jnp.broadcast_to(owned, (count,) + owned.shape), scatter_axis, 0, 0, tiled=False)
    return spread.reshape(-1)[:total]


def per_device(latent, condition, cotangent, expand_kernel, mixing_matrix, project_kernel, offsets):
    planes, x_rows, y_cols = (latent.shape[1], latent.shape[2], latent.shape[3])
    hidden_width = mixing_matrix.shape[0]
    upper_half, lower_half = (latent[:CH], latent[CH:])
    cot_upper, cot_lower = (cotangent[:CH], cotangent[CH:])
    expand_offset = offsets[:hidden_width][:, None, None, None]
    mixing_offset = offsets[hidden_width : 2 * hidden_width][:, None, None, None]
    project_offset = offsets[2 * hidden_width :][:, None, None, None]
    inputs = jnp.concatenate([upper_half.astype(jnp.bfloat16), condition], axis=0)
    wide = frame_cols(extended(inputs, (("gz", 1), ("gx", 2)), 2))
    framed = wide[:, 1:-1, 1:-1]
    pre_wide = forward_taps(wide, expand_kernel, planes + 2, x_rows + 2) + expand_offset
    act_wide = jax.nn.silu(pre_wide).astype(jnp.bfloat16)
    pre_two_wide = (
        jnp.einsum("oc,czxy->ozxy", mixing_matrix, act_wide, preferred_element_type=jnp.float32)
        + mixing_offset
    )
    plane_at = lax.axis_index("gz") * planes - 1 + jnp.arange(planes + 2)
    row_at = lax.axis_index("gx") * x_rows - 1 + jnp.arange(x_rows + 2)
    inside = (
        ((plane_at >= 0) & (plane_at < planes * lax.axis_size("gz")))[:, None]
        & ((row_at >= 0) & (row_at < x_rows * lax.axis_size("gx")))[None, :]
    )
    act_two_wide = jnp.where(inside[None, :, :, None], jax.nn.silu(pre_two_wide), 0.0).astype(jnp.bfloat16)
    act_frame = frame_cols(act_two_wide)
    pre_one = pre_wide[:, 1:-1, 1:-1]
    act_one = act_wide[:, 1:-1, 1:-1]
    pre_two = pre_two_wide[:, 1:-1, 1:-1]
    scores = forward_taps(act_frame, project_kernel, planes, x_rows) + project_offset
    log_scale = jnp.tanh(scores[:CH])
    centered = lower_half - scores[CH:]
    recovered = centered * jnp.exp(-log_scale)
    score_grad = jnp.concatenate(
        [cot_lower * centered * (1.0 - log_scale * log_scale), cot_lower], axis=0
    ).astype(jnp.bfloat16)
    recovered, score_grad, lower_grad = (recovered, score_grad, cot_lower * jnp.exp(log_scale))
    score_frame = frame_cols(extended(score_grad, (("gz", 1), ("gx", 2)), 1))
    hidden_grad = backward_taps(score_frame, project_kernel, planes, x_rows)
    mix_grad = (hidden_grad * silu_slope(pre_two)).astype(jnp.bfloat16)
    back_one = jnp.einsum(
        "oc,ozxy->czxy", mixing_matrix, mix_grad, preferred_element_type=jnp.float32
    )
    first_grad = (back_one * silu_slope(pre_one)).astype(jnp.bfloat16)
    first_frame = frame_cols(extended(first_grad, (("gz", 1), ("gx", 2)), 1))
    input_grad = backward_taps(first_frame, expand_kernel, planes, x_rows)
    inner_first, inner_mix, inner_act = (first_grad, mix_grad, act_one)
    expand_term = weight_taps(inner_first, framed)
    mixing_term = jnp.einsum(
        "ozxy,czxy->oc", inner_mix, inner_act, preferred_element_type=jnp.float32
    )
    project_term = weight_taps(score_grad, act_frame)
    offset_term = jnp.concatenate(
        [channel_sums(inner_first), channel_sums(inner_mix), channel_sums(score_grad)]
    )
    terms = (expand_term, mixing_term, project_term, offset_term)
    flat = replicated_sum(jnp.concatenate([t.reshape(-1) for t in terms]), "gz", ("gx",))
    pieces, start = [], 0
    for t in terms:
        pieces.append(flat[start : start + t.size].reshape(t.shape))
        start += t.size
    expand_sum, mixing_sum, project_sum, offset_sum = pieces
    restored = unsqueeze(jnp.concatenate([upper_half, recovered], axis=0))
    field_grad = unsqueeze(jnp.concatenate([cot_upper + input_grad[:CH], lower_grad], axis=0))
    condition_grad = input_grad[CH:]
    factor = 1.0 / math.sqrt(float(planes * x_rows * y_cols))
    return (
        restored,
        field_grad,
        condition_grad,
        expand_sum * factor,
        mixing_sum * factor,
        project_sum * factor,
        offset_sum * factor,
    )


def solution(mesh):
    placed = (
        P(None, "gz", "gx", None),
        P(None, "gz", "gx", None),
        P(None, "gz", "gx", None),
        P(),
        P(),
        P(),
        P(),
    )
    return jax.shard_map(
        per_device,
        mesh=mesh,
        in_specs=placed,
        out_specs=(
            P("gz", "gx", None),
            P("gz", "gx", None),
            P(None, "gz", "gx", None),
            P(),
            P(),
            P(),
            P(),
        ),
        check_vma=False,
    )
```

```python
import math

import jax
import jax.numpy as jnp
import numpy as np
from jax import lax
from jax.sharding import PartitionSpec as P

CH = 4


def extended(cells, sides, width):
    for axis, dim in sides:
        count = lax.axis_size(axis)
        ends = count - 1
        head = lax.slice_in_dim(cells, 0, width, axis=dim)
        tail = lax.slice_in_dim(cells, cells.shape[dim] - width, cells.shape[dim], axis=dim)
        cells = jnp.concatenate(
            [
                lax.ppermute(tail, axis, [(i, (i + 1) % count) for i in range(ends)]),
                cells,
                lax.ppermute(head, axis, [((i + 1) % count, i) for i in range(ends)]),
            ],
            axis=dim,
        )
    return cells


def set_bits(value):
    parity_count = 0
    for bit_place in range(3):
        parity_count = parity_count + (value >> bit_place & 1)
    return parity_count


def haar_table():
    signs = np.zeros((8, 8), np.float32)
    for fine_index in range(8):
        for coef_index in range(8):
            parity = set_bits(fine_index & coef_index)
            signs[fine_index, coef_index] = (-1.0) ** parity / np.sqrt(8.0)
    return signs


def unsqueeze(coarse):
    haar_signs = jnp.asarray(haar_table())
    spread = jnp.einsum("pk,kzxy->pzxy", haar_signs, coarse, precision=lax.Precision.HIGHEST)
    planes, x_rows, y_cols = (coarse.shape[1], coarse.shape[2], coarse.shape[3])
    spread = spread.reshape(2, 2, 2, planes, x_rows, y_cols).transpose(3, 0, 4, 1, 5, 2)
    return spread.reshape(2 * planes, 2 * x_rows, 2 * y_cols)


def silu_slope(preact):
    sigma = jax.nn.sigmoid(preact)
    return sigma * (1.0 + preact * (1.0 - sigma))


def forward_taps(padded, weight, planes, x_rows):
    y_cols = padded.shape[3] - 2
    summed = None
    for tap_index in range(27):
        z_step, x_step, y_step = (tap_index // 9, tap_index // 3 % 3, tap_index % 3)
        sliced = padded[
            :, z_step : z_step + planes, x_step : x_step + x_rows, y_step : y_step + y_cols
        ]
        product = jnp.einsum(
            "oc,czxy->ozxy", weight[tap_index], sliced, preferred_element_type=jnp.float32
        )
        summed = product if summed is None else summed + product
    return summed


def backward_taps(padded, weight, planes, x_rows):
    y_cols = padded.shape[3] - 2
    summed = None
    for tap_index in range(27):
        z_step, x_step, y_step = (tap_index // 9, tap_index // 3 % 3, tap_index % 3)
        sliced = padded[
            :,
            2 - z_step : 2 - z_step + planes,
            2 - x_step : 2 - x_step + x_rows,
            2 - y_step : 2 - y_step + y_cols,
        ]
        product = jnp.einsum(
            "oc,ozxy->czxy", weight[tap_index], sliced, preferred_element_type=jnp.float32
        )
        summed = product if summed is None else summed + product
    return summed


def weight_taps(grad, padded):
    planes, x_rows, y_cols = (grad.shape[1], grad.shape[2], grad.shape[3])
    result = []
    for tap_index in range(27):
        z_step, x_step, y_step = (tap_index // 9, tap_index // 3 % 3, tap_index % 3)
        sliced = padded[
            :, z_step : z_step + planes, x_step : x_step + x_rows, y_step : y_step + y_cols
        ]
        result.append(jnp.einsum("ozxy,czxy->oc", grad, sliced, preferred_element_type=jnp.float32))
    return jnp.stack(result)


def frame_cols(tensor):
    return jnp.pad(tensor, ((0, 0), (0, 0), (0, 0), (1, 1)))


def channel_sums(tensor):
    return jnp.sum(tensor.astype(jnp.float32), axis=(1, 2, 3))


def butterfly_sum(flat, axes):
    for axis in axes:
        count = lax.axis_size(axis)
        if count & (count - 1):
            flat = lax.psum(flat, axis)
            continue
        bit = 1
        while bit < count:
            flat = flat + lax.ppermute(flat, axis, [(i, i ^ bit) for i in range(count)])
            bit *= 2
    return flat


def replicated_sum(flat, scatter_axis, other_axes):
    total = flat.shape[0]
    count = lax.axis_size(scatter_axis)
    chunks = jnp.pad(flat, (0, (-total) % count)).reshape(count, -1)
    owned = lax.all_to_all(chunks, scatter_axis, 0, 0, tiled=False).sum(0)
    owned = butterfly_sum(owned, other_axes)
    spread = lax.all_to_all(jnp.broadcast_to(owned, (count,) + owned.shape), scatter_axis, 0, 0, tiled=False)
    return spread.reshape(-1)[:total]


def per_device(latent, condition, cotangent, expand_kernel, mixing_matrix, project_kernel, offsets):
    planes, x_rows, y_cols = (latent.shape[1], latent.shape[2], latent.shape[3])
    hidden_width = mixing_matrix.shape[0]
    upper_half, lower_half = (latent[:CH], latent[CH:])
    cot_upper, cot_lower = (cotangent[:CH], cotangent[CH:])
    expand_offset = offsets[:hidden_width][:, None, None, None]
    mixing_offset = offsets[hidden_width : 2 * hidden_width][:, None, None, None]
    project_offset = offsets[2 * hidden_width :][:, None, None, None]
    inputs = jnp.concatenate([upper_half.astype(jnp.bfloat16), condition], axis=0)
    wide = frame_cols(extended(inputs, (("gz", 1), ("gx", 2)), 2))
    framed = wide[:, 1:-1, 1:-1]
    pre_wide = forward_taps(wide, expand_kernel, planes + 2, x_rows + 2) + expand_offset
    act_wide = jax.nn.silu(pre_wide).astype(jnp.bfloat16)
    pre_two_wide = (
        jnp.einsum("oc,czxy->ozxy", mixing_matrix, act_wide, preferred_element_type=jnp.float32)
        + mixing_offset
    )
    plane_at = lax.axis_index("gz") * planes - 1 + jnp.arange(planes + 2)
    row_at = lax.axis_index("gx") * x_rows - 1 + jnp.arange(x_rows + 2)
    inside = (
        ((plane_at >= 0) & (plane_at < planes * lax.axis_size("gz")))[:, None]
        & ((row_at >= 0) & (row_at < x_rows * lax.axis_size("gx")))[None, :]
    )
    act_two_wide = jnp.where(inside[None, :, :, None], jax.nn.silu(pre_two_wide), 0.0).astype(jnp.bfloat16)
    act_frame = frame_cols(act_two_wide)
    pre_one = pre_wide[:, 1:-1, 1:-1]
    act_one = act_wide[:, 1:-1, 1:-1]
    pre_two = pre_two_wide[:, 1:-1, 1:-1]
    scores = forward_taps(act_frame, project_kernel, planes, x_rows) + project_offset
    log_scale = jnp.tanh(scores[:CH])
    centered = lower_half - scores[CH:]
    recovered = centered * jnp.exp(-log_scale)
    score_grad = jnp.concatenate(
        [cot_lower * centered * (1.0 - log_scale * log_scale), cot_lower], axis=0
    ).astype(jnp.bfloat16)
    recovered, score_grad, lower_grad = (recovered, score_grad, cot_lower * jnp.exp(log_scale))
    score_frame = frame_cols(extended(score_grad, (("gz", 1), ("gx", 2)), 1))
    hidden_grad = backward_taps(score_frame, project_kernel, planes, x_rows)
    mix_grad = (hidden_grad * silu_slope(pre_two)).astype(jnp.bfloat16)
    back_one = jnp.einsum(
        "oc,ozxy->czxy", mixing_matrix, mix_grad, preferred_element_type=jnp.float32
    )
    first_grad = (back_one * silu_slope(pre_one)).astype(jnp.bfloat16)
    inner_first, inner_mix, inner_act = (first_grad, mix_grad, act_one)
    expand_term = weight_taps(inner_first, framed)
    mixing_term = jnp.einsum(
        "ozxy,czxy->oc", inner_mix, inner_act, preferred_element_type=jnp.float32
    )
    project_term = weight_taps(score_grad, act_frame)
    offset_term = jnp.concatenate(
        [channel_sums(inner_first), channel_sums(inner_mix), channel_sums(score_grad)]
    )
    terms = (expand_term, mixing_term, project_term, offset_term)
    flat = jnp.concatenate([t.reshape(-1) for t in terms])
    total = flat.shape[0]
    count = lax.axis_size("gz")
    chunks = jnp.pad(flat, (0, (-total) % count)).reshape(count, -1)
    owned = lax.all_to_all(chunks, "gz", 0, 0, tiled=False).sum(0)
    owned, first_grad = lax.optimization_barrier((owned, first_grad))
    owned = butterfly_sum(owned, ("gx",))
    first_frame = frame_cols(extended(first_grad, (("gz", 1), ("gx", 2)), 1))
    input_grad = backward_taps(first_frame, expand_kernel, planes, x_rows)
    spread = lax.all_to_all(jnp.broadcast_to(owned, (count,) + owned.shape), "gz", 0, 0, tiled=False)
    flat = spread.reshape(-1)[:total]
    pieces, start = [], 0
    for t in terms:
        pieces.append(flat[start : start + t.size].reshape(t.shape))
        start += t.size
    expand_sum, mixing_sum, project_sum, offset_sum = pieces
    restored = unsqueeze(jnp.concatenate([upper_half, recovered], axis=0))
    field_grad = unsqueeze(jnp.concatenate([cot_upper + input_grad[:CH], lower_grad], axis=0))
    condition_grad = input_grad[CH:]
    factor = 1.0 / math.sqrt(float(planes * x_rows * y_cols))
    return (
        restored,
        field_grad,
        condition_grad,
        expand_sum * factor,
        mixing_sum * factor,
        project_sum * factor,
        offset_sum * factor,
    )


def solution(mesh):
    placed = (
        P(None, "gz", "gx", None),
        P(None, "gz", "gx", None),
        P(None, "gz", "gx", None),
        P(),
        P(),
        P(),
        P(),
    )
    return jax.shard_map(
        per_device,
        mesh=mesh,
        in_specs=placed,
        out_specs=(
            P("gz", "gx", None),
            P("gz", "gx", None),
            P(None, "gz", "gx", None),
            P(),
            P(),
            P(),
            P(),
        ),
        check_vma=False,
    )
```

```python
import math

import jax
import jax.numpy as jnp
import numpy as np
from jax import lax
from jax.sharding import PartitionSpec as P

CH = 4


def extended(cells, sides, width):
    for axis, dim in sides:
        count = lax.axis_size(axis)
        ends = count - 1
        head = lax.slice_in_dim(cells, 0, width, axis=dim)
        tail = lax.slice_in_dim(cells, cells.shape[dim] - width, cells.shape[dim], axis=dim)
        cells = jnp.concatenate(
            [
                lax.ppermute(tail, axis, [(i, (i + 1) % count) for i in range(ends)]),
                cells,
                lax.ppermute(head, axis, [((i + 1) % count, i) for i in range(ends)]),
            ],
            axis=dim,
        )
    return cells


def set_bits(value):
    parity_count = 0
    for bit_place in range(3):
        parity_count = parity_count + (value >> bit_place & 1)
    return parity_count


def haar_table():
    signs = np.zeros((8, 8), np.float32)
    for fine_index in range(8):
        for coef_index in range(8):
            parity = set_bits(fine_index & coef_index)
            signs[fine_index, coef_index] = (-1.0) ** parity / np.sqrt(8.0)
    return signs


def unsqueeze(coarse):
    haar_signs = jnp.asarray(haar_table())
    spread = jnp.einsum("pk,kzxy->pzxy", haar_signs, coarse, precision=lax.Precision.HIGHEST)
    planes, x_rows, y_cols = (coarse.shape[1], coarse.shape[2], coarse.shape[3])
    spread = spread.reshape(2, 2, 2, planes, x_rows, y_cols).transpose(3, 0, 4, 1, 5, 2)
    return spread.reshape(2 * planes, 2 * x_rows, 2 * y_cols)


def silu_slope(preact):
    sigma = jax.nn.sigmoid(preact)
    return sigma * (1.0 + preact * (1.0 - sigma))


def shifted(padded, planes, x_rows, flip):
    y_cols = padded.shape[3] - 2
    slices = []
    for tap_index in range(27):
        z_step, x_step, y_step = (tap_index // 9, tap_index // 3 % 3, tap_index % 3)
        if flip:
            z_step, x_step, y_step = (2 - z_step, 2 - x_step, 2 - y_step)
        slices.append(
            padded[:, z_step : z_step + planes, x_step : x_step + x_rows, y_step : y_step + y_cols]
        )
    return jnp.stack(slices)


def forward_taps(padded, weight, planes, x_rows):
    return jnp.einsum(
        "toc,tczxy->ozxy", weight, shifted(padded, planes, x_rows, False),
        preferred_element_type=jnp.float32,
    )


def backward_taps(padded, weight, planes, x_rows):
    return jnp.einsum(
        "toc,tozxy->czxy", weight, shifted(padded, planes, x_rows, True),
        preferred_element_type=jnp.float32,
    )


def weight_taps(grad, padded):
    planes, x_rows = (grad.shape[1], grad.shape[2])
    return jnp.einsum(
        "ozxy,tczxy->toc", grad, shifted(padded, planes, x_rows, False),
        preferred_element_type=jnp.float32,
    )


def frame_cols(tensor):
    return jnp.pad(tensor, ((0, 0), (0, 0), (0, 0), (1, 1)))


def channel_sums(tensor):
    return jnp.sum(tensor.astype(jnp.float32), axis=(1, 2, 3))


def butterfly_sum(flat, axes):
    for axis in axes:
        count = lax.axis_size(axis)
        if count & (count - 1):
            flat = lax.psum(flat, axis)
            continue
        bit = 1
        while bit < count:
            flat = flat + lax.ppermute(flat, axis, [(i, i ^ bit) for i in range(count)])
            bit *= 2
    return flat


def replicated_sum(flat, scatter_axis, other_axes):
    total = flat.shape[0]
    count = lax.axis_size(scatter_axis)
    chunks = jnp.pad(flat, (0, (-total) % count)).reshape(count, -1)
    owned = lax.all_to_all(chunks, scatter_axis, 0, 0, tiled=False).sum(0)
    owned = butterfly_sum(owned, other_axes)
    spread = lax.all_to_all(jnp.broadcast_to(owned, (count,) + owned.shape), scatter_axis, 0, 0, tiled=False)
    return spread.reshape(-1)[:total]


def per_device(latent, condition, cotangent, expand_kernel, mixing_matrix, project_kernel, offsets):
    planes, x_rows, y_cols = (latent.shape[1], latent.shape[2], latent.shape[3])
    hidden_width = mixing_matrix.shape[0]
    upper_half, lower_half = (latent[:CH], latent[CH:])
    cot_upper, cot_lower = (cotangent[:CH], cotangent[CH:])
    expand_offset = offsets[:hidden_width][:, None, None, None]
    mixing_offset = offsets[hidden_width : 2 * hidden_width][:, None, None, None]
    project_offset = offsets[2 * hidden_width :][:, None, None, None]
    inputs = jnp.concatenate([upper_half.astype(jnp.bfloat16), condition], axis=0)
    wide = frame_cols(extended(inputs, (("gz", 1), ("gx", 2)), 2))
    framed = wide[:, 1:-1, 1:-1]
    pre_wide = forward_taps(wide, expand_kernel, planes + 2, x_rows + 2) + expand_offset
    act_wide = jax.nn.silu(pre_wide).astype(jnp.bfloat16)
    pre_two_wide = (
        jnp.einsum("oc,czxy->ozxy", mixing_matrix, act_wide, preferred_element_type=jnp.float32)
        + mixing_offset
    )
    plane_at = lax.axis_index("gz") * planes - 1 + jnp.arange(planes + 2)
    row_at = lax.axis_index("gx") * x_rows - 1 + jnp.arange(x_rows + 2)
    inside = (
        ((plane_at >= 0) & (plane_at < planes * lax.axis_size("gz")))[:, None]
        & ((row_at >= 0) & (row_at < x_rows * lax.axis_size("gx")))[None, :]
    )
    act_two_wide = jnp.where(inside[None, :, :, None], jax.nn.silu(pre_two_wide), 0.0).astype(jnp.bfloat16)
    act_frame = frame_cols(act_two_wide)
    pre_one = pre_wide[:, 1:-1, 1:-1]
    act_one = act_wide[:, 1:-1, 1:-1]
    pre_two = pre_two_wide[:, 1:-1, 1:-1]
    scores = forward_taps(act_frame, project_kernel, planes, x_rows) + project_offset
    log_scale = jnp.tanh(scores[:CH])
    centered = lower_half - scores[CH:]
    recovered = centered * jnp.exp(-log_scale)
    score_grad = jnp.concatenate(
        [cot_lower * centered * (1.0 - log_scale * log_scale), cot_lower], axis=0
    ).astype(jnp.bfloat16)
    recovered, score_grad, lower_grad = (recovered, score_grad, cot_lower * jnp.exp(log_scale))
    score_frame = frame_cols(extended(score_grad, (("gz", 1), ("gx", 2)), 1))
    hidden_grad = backward_taps(score_frame, project_kernel, planes, x_rows)
    mix_grad = (hidden_grad * silu_slope(pre_two)).astype(jnp.bfloat16)
    back_one = jnp.einsum(
        "oc,ozxy->czxy", mixing_matrix, mix_grad, preferred_element_type=jnp.float32
    )
    first_grad = (back_one * silu_slope(pre_one)).astype(jnp.bfloat16)
    inner_first, inner_mix, inner_act = (first_grad, mix_grad, act_one)
    expand_term = weight_taps(inner_first, framed)
    mixing_term = jnp.einsum(
        "ozxy,czxy->oc", inner_mix, inner_act, preferred_element_type=jnp.float32
    )
    project_term = weight_taps(score_grad, act_frame)
    offset_term = jnp.concatenate(
        [channel_sums(inner_first), channel_sums(inner_mix), channel_sums(score_grad)]
    )
    terms = (expand_term, mixing_term, project_term, offset_term)
    flat = jnp.concatenate([t.reshape(-1) for t in terms])
    total = flat.shape[0]
    count = lax.axis_size("gz")
    chunks = jnp.pad(flat, (0, (-total) % count)).reshape(count, -1)
    owned = lax.all_to_all(chunks, "gz", 0, 0, tiled=False).sum(0)
    owned, first_grad = lax.optimization_barrier((owned, first_grad))
    owned = butterfly_sum(owned, ("gx",))
    first_frame = frame_cols(extended(first_grad, (("gz", 1), ("gx", 2)), 1))
    input_grad = backward_taps(first_frame, expand_kernel, planes, x_rows)
    spread = lax.all_to_all(jnp.broadcast_to(owned, (count,) + owned.shape), "gz", 0, 0, tiled=False)
    flat = spread.reshape(-1)[:total]
    pieces, start = [], 0
    for t in terms:
        pieces.append(flat[start : start + t.size].reshape(t.shape))
        start += t.size
    expand_sum, mixing_sum, project_sum, offset_sum = pieces
    restored = unsqueeze(jnp.concatenate([upper_half, recovered], axis=0))
    field_grad = unsqueeze(jnp.concatenate([cot_upper + input_grad[:CH], lower_grad], axis=0))
    condition_grad = input_grad[CH:]
    factor = 1.0 / math.sqrt(float(planes * x_rows * y_cols))
    return (
        restored,
        field_grad,
        condition_grad,
        expand_sum * factor,
        mixing_sum * factor,
        project_sum * factor,
        offset_sum * factor,
    )


def solution(mesh):
    placed = (
        P(None, "gz", "gx", None),
        P(None, "gz", "gx", None),
        P(None, "gz", "gx", None),
        P(),
        P(),
        P(),
        P(),
    )
    return jax.shard_map(
        per_device,
        mesh=mesh,
        in_specs=placed,
        out_specs=(
            P("gz", "gx", None),
            P("gz", "gx", None),
            P(None, "gz", "gx", None),
            P(),
            P(),
            P(),
            P(),
        ),
        check_vma=False,
    )
```

```python
import math

import jax
import jax.numpy as jnp
import numpy as np
from jax import lax
from jax.sharding import PartitionSpec as P

CH = 4


def extended(cells, sides, width):
    for axis, dim in sides:
        count = lax.axis_size(axis)
        ends = count - 1
        head = lax.slice_in_dim(cells, 0, width, axis=dim)
        tail = lax.slice_in_dim(cells, cells.shape[dim] - width, cells.shape[dim], axis=dim)
        cells = jnp.concatenate(
            [
                lax.ppermute(tail, axis, [(i, (i + 1) % count) for i in range(ends)]),
                cells,
                lax.ppermute(head, axis, [((i + 1) % count, i) for i in range(ends)]),
            ],
            axis=dim,
        )
    return cells


def set_bits(value):
    parity_count = 0
    for bit_place in range(3):
        parity_count = parity_count + (value >> bit_place & 1)
    return parity_count


def haar_table():
    signs = np.zeros((8, 8), np.float32)
    for fine_index in range(8):
        for coef_index in range(8):
            parity = set_bits(fine_index & coef_index)
            signs[fine_index, coef_index] = (-1.0) ** parity / np.sqrt(8.0)
    return signs


def unsqueeze(coarse):
    haar_signs = jnp.asarray(haar_table())
    spread = jnp.einsum("pk,kzxy->pzxy", haar_signs, coarse, precision=lax.Precision.HIGHEST)
    planes, x_rows, y_cols = (coarse.shape[1], coarse.shape[2], coarse.shape[3])
    spread = spread.reshape(2, 2, 2, planes, x_rows, y_cols).transpose(3, 0, 4, 1, 5, 2)
    return spread.reshape(2 * planes, 2 * x_rows, 2 * y_cols)


def silu_slope(preact):
    sigma = jax.nn.sigmoid(preact)
    return sigma * (1.0 + preact * (1.0 - sigma))


def forward_taps(padded, weight, planes, x_rows):
    y_cols = padded.shape[3] - 2
    summed = None
    for tap_index in range(27):
        z_step, x_step, y_step = (tap_index // 9, tap_index // 3 % 3, tap_index % 3)
        sliced = padded[
            :, z_step : z_step + planes, x_step : x_step + x_rows, y_step : y_step + y_cols
        ]
        product = jnp.einsum(
            "oc,czxy->ozxy", weight[tap_index], sliced, preferred_element_type=jnp.float32
        )
        summed = product if summed is None else summed + product
    return summed


def backward_taps(padded, weight, planes, x_rows):
    y_cols = padded.shape[3] - 2
    summed = None
    for tap_index in range(27):
        z_step, x_step, y_step = (tap_index // 9, tap_index // 3 % 3, tap_index % 3)
        sliced = padded[
            :,
            2 - z_step : 2 - z_step + planes,
            2 - x_step : 2 - x_step + x_rows,
            2 - y_step : 2 - y_step + y_cols,
        ]
        product = jnp.einsum(
            "oc,ozxy->czxy", weight[tap_index], sliced, preferred_element_type=jnp.float32
        )
        summed = product if summed is None else summed + product
    return summed


def weight_taps(grad, padded):
    planes, x_rows, y_cols = (grad.shape[1], grad.shape[2], grad.shape[3])
    result = []
    for tap_index in range(27):
        z_step, x_step, y_step = (tap_index // 9, tap_index // 3 % 3, tap_index % 3)
        sliced = padded[
            :, z_step : z_step + planes, x_step : x_step + x_rows, y_step : y_step + y_cols
        ]
        result.append(jnp.einsum("ozxy,czxy->oc", grad, sliced, preferred_element_type=jnp.float32))
    return jnp.stack(result)


def frame_cols(tensor):
    return jnp.pad(tensor, ((0, 0), (0, 0), (0, 0), (1, 1)))


def channel_sums(tensor):
    return jnp.sum(tensor.astype(jnp.float32), axis=(1, 2, 3))


def butterfly_sum(flat, axes):
    for axis in axes:
        count = lax.axis_size(axis)
        if count & (count - 1):
            flat = lax.psum(flat, axis)
            continue
        bit = 1
        while bit < count:
            flat = flat + lax.ppermute(flat, axis, [(i, i ^ bit) for i in range(count)])
            bit *= 2
    return flat


def replicated_sum(flat, scatter_axis, other_axes):
    total = flat.shape[0]
    count = lax.axis_size(scatter_axis)
    chunks = jnp.pad(flat, (0, (-total) % count)).reshape(count, -1)
    owned = lax.all_to_all(chunks, scatter_axis, 0, 0, tiled=False).sum(0)
    owned = butterfly_sum(owned, other_axes)
    spread = lax.all_to_all(jnp.broadcast_to(owned, (count,) + owned.shape), scatter_axis, 0, 0, tiled=False)
    return spread.reshape(-1)[:total]


def per_device(latent, condition, cotangent, expand_kernel, mixing_matrix, project_kernel, offsets):
    planes, x_rows, y_cols = (latent.shape[1], latent.shape[2], latent.shape[3])
    hidden_width = mixing_matrix.shape[0]
    upper_half, lower_half = (latent[:CH], latent[CH:])
    cot_upper, cot_lower = (cotangent[:CH], cotangent[CH:])
    expand_offset = offsets[:hidden_width][:, None, None, None]
    mixing_offset = offsets[hidden_width : 2 * hidden_width][:, None, None, None]
    project_offset = offsets[2 * hidden_width :][:, None, None, None]
    inputs = jnp.concatenate([upper_half.astype(jnp.bfloat16), condition], axis=0)
    wide = frame_cols(extended(inputs, (("gz", 1), ("gx", 2)), 2))
    framed = wide[:, 1:-1, 1:-1]
    pre_wide = forward_taps(wide, expand_kernel, planes + 2, x_rows + 2) + expand_offset
    act_wide = jax.nn.silu(pre_wide).astype(jnp.bfloat16)
    pre_two_wide = (
        jnp.einsum("oc,czxy->ozxy", mixing_matrix, act_wide, preferred_element_type=jnp.float32)
        + mixing_offset
    )
    plane_at = lax.axis_index("gz") * planes - 1 + jnp.arange(planes + 2)
    row_at = lax.axis_index("gx") * x_rows - 1 + jnp.arange(x_rows + 2)
    inside = (
        ((plane_at >= 0) & (plane_at < planes * lax.axis_size("gz")))[:, None]
        & ((row_at >= 0) & (row_at < x_rows * lax.axis_size("gx")))[None, :]
    )
    act_two_wide = jnp.where(inside[None, :, :, None], jax.nn.silu(pre_two_wide), 0.0).astype(jnp.bfloat16)
    act_frame = frame_cols(act_two_wide)
    pre_one = pre_wide[:, 1:-1, 1:-1]
    act_one = act_wide[:, 1:-1, 1:-1]
    pre_two = pre_two_wide[:, 1:-1, 1:-1]
    scores = forward_taps(act_frame, project_kernel, planes, x_rows) + project_offset
    log_scale = jnp.tanh(scores[:CH])
    centered = lower_half - scores[CH:]
    recovered = centered * jnp.exp(-log_scale)
    score_grad = jnp.concatenate(
        [cot_lower * centered * (1.0 - log_scale * log_scale), cot_lower], axis=0
    ).astype(jnp.bfloat16)
    recovered, score_grad, lower_grad = (recovered, score_grad, cot_lower * jnp.exp(log_scale))
    score_frame = frame_cols(extended(score_grad, (("gz", 1), ("gx", 2)), 1))
    hidden_grad = backward_taps(score_frame, project_kernel, planes, x_rows)
    mix_grad = (hidden_grad * silu_slope(pre_two)).astype(jnp.bfloat16)
    back_one = jnp.einsum(
        "oc,ozxy->czxy", mixing_matrix, mix_grad, preferred_element_type=jnp.float32
    )
    first_grad = (back_one * silu_slope(pre_one)).astype(jnp.bfloat16)
    inner_first, inner_mix, inner_act = (first_grad, mix_grad, act_one)
    expand_term = weight_taps(inner_first, framed)
    mixing_term = jnp.einsum(
        "ozxy,czxy->oc", inner_mix, inner_act, preferred_element_type=jnp.float32
    )
    project_term = weight_taps(score_grad, act_frame)
    offset_term = jnp.concatenate(
        [channel_sums(inner_first), channel_sums(inner_mix), channel_sums(score_grad)]
    )
    terms = (expand_term, mixing_term, project_term, offset_term)
    flat = jnp.concatenate([t.reshape(-1) for t in terms])
    total = flat.shape[0]
    count = lax.axis_size("gz")
    chunks = jnp.pad(flat, (0, (-total) % count)).reshape(count, -1)
    owned = lax.all_to_all(chunks, "gz", 0, 0, tiled=False).sum(0)
    owned, first_grad = lax.optimization_barrier((owned, first_grad))
    factor = 1.0 / math.sqrt(float(planes * x_rows * y_cols))
    owned = butterfly_sum(owned, ("gx",)) * factor
    first_frame = frame_cols(extended(first_grad, (("gz", 1), ("gx", 2)), 1))
    input_grad = backward_taps(first_frame, expand_kernel, planes, x_rows)
    spread = lax.all_to_all(jnp.broadcast_to(owned, (count,) + owned.shape), "gz", 0, 0, tiled=False)
    flat = spread.reshape(-1)[:total]
    pieces, start = [], 0
    for t in terms:
        pieces.append(flat[start : start + t.size].reshape(t.shape))
        start += t.size
    expand_sum, mixing_sum, project_sum, offset_sum = pieces
    restored = unsqueeze(jnp.concatenate([upper_half, recovered], axis=0))
    field_grad = unsqueeze(jnp.concatenate([cot_upper + input_grad[:CH], lower_grad], axis=0))
    condition_grad = input_grad[CH:]
    return (
        restored,
        field_grad,
        condition_grad,
        expand_sum,
        mixing_sum,
        project_sum,
        offset_sum,
    )


def solution(mesh):
    placed = (
        P(None, "gz", "gx", None),
        P(None, "gz", "gx", None),
        P(None, "gz", "gx", None),
        P(),
        P(),
        P(),
        P(),
    )
    return jax.shard_map(
        per_device,
        mesh=mesh,
        in_specs=placed,
        out_specs=(
            P("gz", "gx", None),
            P("gz", "gx", None),
            P(None, "gz", "gx", None),
            P(),
            P(),
            P(),
            P(),
        ),
        check_vma=False,
    )
```

```python
import math

import jax
import jax.numpy as jnp
import numpy as np
from jax import lax
from jax.sharding import PartitionSpec as P

CH = 4


def extended(cells, sides, width):
    for axis, dim in sides:
        count = lax.axis_size(axis)
        ends = count - 1
        head = lax.slice_in_dim(cells, 0, width, axis=dim)
        tail = lax.slice_in_dim(cells, cells.shape[dim] - width, cells.shape[dim], axis=dim)
        cells = jnp.concatenate(
            [
                lax.ppermute(tail, axis, [(i, (i + 1) % count) for i in range(ends)]),
                cells,
                lax.ppermute(head, axis, [((i + 1) % count, i) for i in range(ends)]),
            ],
            axis=dim,
        )
    return cells


def set_bits(value):
    parity_count = 0
    for bit_place in range(3):
        parity_count = parity_count + (value >> bit_place & 1)
    return parity_count


def haar_table():
    signs = np.zeros((8, 8), np.float32)
    for fine_index in range(8):
        for coef_index in range(8):
            parity = set_bits(fine_index & coef_index)
            signs[fine_index, coef_index] = (-1.0) ** parity / np.sqrt(8.0)
    return signs


def unsqueeze(coarse):
    haar_signs = jnp.asarray(haar_table())
    spread = jnp.einsum("pk,kzxy->pzxy", haar_signs, coarse, precision=lax.Precision.HIGHEST)
    planes, x_rows, y_cols = (coarse.shape[1], coarse.shape[2], coarse.shape[3])
    spread = spread.reshape(2, 2, 2, planes, x_rows, y_cols).transpose(3, 0, 4, 1, 5, 2)
    return spread.reshape(2 * planes, 2 * x_rows, 2 * y_cols)


def silu_slope(preact):
    sigma = jax.nn.sigmoid(preact)
    return sigma * (1.0 + preact * (1.0 - sigma))


def y_shifts(padded):
    y_cols = padded.shape[3] - 2
    return jnp.stack([padded[..., y_step : y_step + y_cols] for y_step in range(3)])


def forward_taps(padded, weight, planes, x_rows):
    stacked = y_shifts(padded)
    kernel = weight.reshape((3, 3, 3) + weight.shape[1:])
    summed = None
    for z_step in range(3):
        for x_step in range(3):
            product = jnp.einsum(
                "eoc,eczxy->ozxy",
                kernel[z_step, x_step],
                stacked[:, :, z_step : z_step + planes, x_step : x_step + x_rows],
                preferred_element_type=jnp.float32,
            )
            summed = product if summed is None else summed + product
    return summed


def backward_taps(padded, weight, planes, x_rows):
    stacked = y_shifts(padded)
    kernel = weight.reshape((3, 3, 3) + weight.shape[1:])
    summed = None
    for z_step in range(3):
        for x_step in range(3):
            product = jnp.einsum(
                "eoc,eozxy->czxy",
                kernel[z_step, x_step, ::-1],
                stacked[:, :, 2 - z_step : 2 - z_step + planes, 2 - x_step : 2 - x_step + x_rows],
                preferred_element_type=jnp.float32,
            )
            summed = product if summed is None else summed + product
    return summed


def weight_taps(grad, padded):
    planes, x_rows = (grad.shape[1], grad.shape[2])
    stacked = y_shifts(padded)
    result = []
    for z_step in range(3):
        for x_step in range(3):
            result.append(
                jnp.einsum(
                    "ozxy,eczxy->eoc",
                    grad,
                    stacked[:, :, z_step : z_step + planes, x_step : x_step + x_rows],
                    preferred_element_type=jnp.float32,
                )
            )
    return jnp.concatenate(result)


def frame_cols(tensor):
    return jnp.pad(tensor, ((0, 0), (0, 0), (0, 0), (1, 1)))


def channel_sums(tensor):
    return jnp.sum(tensor.astype(jnp.float32), axis=(1, 2, 3))


def butterfly_sum(flat, axes):
    for axis in axes:
        count = lax.axis_size(axis)
        if count & (count - 1):
            flat = lax.psum(flat, axis)
            continue
        bit = 1
        while bit < count:
            flat = flat + lax.ppermute(flat, axis, [(i, i ^ bit) for i in range(count)])
            bit *= 2
    return flat


def replicated_sum(flat, scatter_axis, other_axes):
    total = flat.shape[0]
    count = lax.axis_size(scatter_axis)
    chunks = jnp.pad(flat, (0, (-total) % count)).reshape(count, -1)
    owned = lax.all_to_all(chunks, scatter_axis, 0, 0, tiled=False).sum(0)
    owned = butterfly_sum(owned, other_axes)
    spread = lax.all_to_all(jnp.broadcast_to(owned, (count,) + owned.shape), scatter_axis, 0, 0, tiled=False)
    return spread.reshape(-1)[:total]


def per_device(latent, condition, cotangent, expand_kernel, mixing_matrix, project_kernel, offsets):
    planes, x_rows, y_cols = (latent.shape[1], latent.shape[2], latent.shape[3])
    hidden_width = mixing_matrix.shape[0]
    upper_half, lower_half = (latent[:CH], latent[CH:])
    cot_upper, cot_lower = (cotangent[:CH], cotangent[CH:])
    expand_offset = offsets[:hidden_width][:, None, None, None]
    mixing_offset = offsets[hidden_width : 2 * hidden_width][:, None, None, None]
    project_offset = offsets[2 * hidden_width :][:, None, None, None]
    inputs = jnp.concatenate([upper_half.astype(jnp.bfloat16), condition], axis=0)
    wide = frame_cols(extended(inputs, (("gz", 1), ("gx", 2)), 2))
    framed = wide[:, 1:-1, 1:-1]
    pre_wide = forward_taps(wide, expand_kernel, planes + 2, x_rows + 2) + expand_offset
    act_wide = jax.nn.silu(pre_wide).astype(jnp.bfloat16)
    pre_two_wide = (
        jnp.einsum("oc,czxy->ozxy", mixing_matrix, act_wide, preferred_element_type=jnp.float32)
        + mixing_offset
    )
    plane_at = lax.axis_index("gz") * planes - 1 + jnp.arange(planes + 2)
    row_at = lax.axis_index("gx") * x_rows - 1 + jnp.arange(x_rows + 2)
    inside = (
        ((plane_at >= 0) & (plane_at < planes * lax.axis_size("gz")))[:, None]
        & ((row_at >= 0) & (row_at < x_rows * lax.axis_size("gx")))[None, :]
    )
    act_two_wide = jnp.where(inside[None, :, :, None], jax.nn.silu(pre_two_wide), 0.0).astype(jnp.bfloat16)
    act_frame = frame_cols(act_two_wide)
    pre_one = pre_wide[:, 1:-1, 1:-1]
    act_one = act_wide[:, 1:-1, 1:-1]
    pre_two = pre_two_wide[:, 1:-1, 1:-1]
    scores = forward_taps(act_frame, project_kernel, planes, x_rows) + project_offset
    log_scale = jnp.tanh(scores[:CH])
    centered = lower_half - scores[CH:]
    recovered = centered * jnp.exp(-log_scale)
    score_grad = jnp.concatenate(
        [cot_lower * centered * (1.0 - log_scale * log_scale), cot_lower], axis=0
    ).astype(jnp.bfloat16)
    recovered, score_grad, lower_grad = (recovered, score_grad, cot_lower * jnp.exp(log_scale))
    score_frame = frame_cols(extended(score_grad, (("gz", 1), ("gx", 2)), 1))
    hidden_grad = backward_taps(score_frame, project_kernel, planes, x_rows)
    mix_grad = (hidden_grad * silu_slope(pre_two)).astype(jnp.bfloat16)
    back_one = jnp.einsum(
        "oc,ozxy->czxy", mixing_matrix, mix_grad, preferred_element_type=jnp.float32
    )
    first_grad = (back_one * silu_slope(pre_one)).astype(jnp.bfloat16)
    inner_first, inner_mix, inner_act = (first_grad, mix_grad, act_one)
    expand_term = weight_taps(inner_first, framed)
    mixing_term = jnp.einsum(
        "ozxy,czxy->oc", inner_mix, inner_act, preferred_element_type=jnp.float32
    )
    project_term = weight_taps(score_grad, act_frame)
    offset_term = jnp.concatenate(
        [channel_sums(inner_first), channel_sums(inner_mix), channel_sums(score_grad)]
    )
    terms = (expand_term, mixing_term, project_term, offset_term)
    flat = jnp.concatenate([t.reshape(-1) for t in terms])
    total = flat.shape[0]
    count = lax.axis_size("gz")
    chunks = jnp.pad(flat, (0, (-total) % count)).reshape(count, -1)
    owned = lax.all_to_all(chunks, "gz", 0, 0, tiled=False).sum(0)
    owned, first_grad = lax.optimization_barrier((owned, first_grad))
    factor = 1.0 / math.sqrt(float(planes * x_rows * y_cols))
    owned = butterfly_sum(owned, ("gx",)) * factor
    first_frame = frame_cols(extended(first_grad, (("gz", 1), ("gx", 2)), 1))
    input_grad = backward_taps(first_frame, expand_kernel, planes, x_rows)
    spread = lax.all_to_all(jnp.broadcast_to(owned, (count,) + owned.shape), "gz", 0, 0, tiled=False)
    flat = spread.reshape(-1)[:total]
    pieces, start = [], 0
    for t in terms:
        pieces.append(flat[start : start + t.size].reshape(t.shape))
        start += t.size
    expand_sum, mixing_sum, project_sum, offset_sum = pieces
    restored = unsqueeze(jnp.concatenate([upper_half, recovered], axis=0))
    field_grad = unsqueeze(jnp.concatenate([cot_upper + input_grad[:CH], lower_grad], axis=0))
    condition_grad = input_grad[CH:]
    return (
        restored,
        field_grad,
        condition_grad,
        expand_sum,
        mixing_sum,
        project_sum,
        offset_sum,
    )


def solution(mesh):
    placed = (
        P(None, "gz", "gx", None),
        P(None, "gz", "gx", None),
        P(None, "gz", "gx", None),
        P(),
        P(),
        P(),
        P(),
    )
    return jax.shard_map(
        per_device,
        mesh=mesh,
        in_specs=placed,
        out_specs=(
            P("gz", "gx", None),
            P("gz", "gx", None),
            P(None, "gz", "gx", None),
            P(),
            P(),
            P(),
            P(),
        ),
        check_vma=False,
    )
```

```python
import math

import jax
import jax.numpy as jnp
import numpy as np
from jax import lax
from jax.sharding import PartitionSpec as P

CH = 4


def extended(cells, sides, width):
    for axis, dim in sides:
        count = lax.axis_size(axis)
        ends = count - 1
        head = lax.slice_in_dim(cells, 0, width, axis=dim)
        tail = lax.slice_in_dim(cells, cells.shape[dim] - width, cells.shape[dim], axis=dim)
        cells = jnp.concatenate(
            [
                lax.ppermute(tail, axis, [(i, (i + 1) % count) for i in range(ends)]),
                cells,
                lax.ppermute(head, axis, [((i + 1) % count, i) for i in range(ends)]),
            ],
            axis=dim,
        )
    return cells


def set_bits(value):
    parity_count = 0
    for bit_place in range(3):
        parity_count = parity_count + (value >> bit_place & 1)
    return parity_count


def haar_table():
    signs = np.zeros((8, 8), np.float32)
    for fine_index in range(8):
        for coef_index in range(8):
            parity = set_bits(fine_index & coef_index)
            signs[fine_index, coef_index] = (-1.0) ** parity / np.sqrt(8.0)
    return signs


def unsqueeze(coarse):
    haar_signs = jnp.asarray(haar_table())
    spread = jnp.einsum("pk,kzxy->pzxy", haar_signs, coarse, precision=lax.Precision.HIGHEST)
    planes, x_rows, y_cols = (coarse.shape[1], coarse.shape[2], coarse.shape[3])
    spread = spread.reshape(2, 2, 2, planes, x_rows, y_cols).transpose(3, 0, 4, 1, 5, 2)
    return spread.reshape(2 * planes, 2 * x_rows, 2 * y_cols)


def silu_slope(preact):
    sigma = jax.nn.sigmoid(preact)
    return sigma * (1.0 + preact * (1.0 - sigma))


def y_shifts(padded):
    y_cols = padded.shape[3] - 2
    return jnp.stack([padded[..., y_step : y_step + y_cols] for y_step in range(3)])


def forward_taps(padded, weight, planes, x_rows):
    stacked = y_shifts(padded)
    kernel = weight.reshape((3, 3, 3) + weight.shape[1:])
    summed = None
    for z_step in range(3):
        for x_step in range(3):
            product = jnp.einsum(
                "eoc,eczxy->ozxy",
                kernel[z_step, x_step],
                stacked[:, :, z_step : z_step + planes, x_step : x_step + x_rows],
                preferred_element_type=jnp.float32,
            )
            summed = product if summed is None else summed + product
    return summed


def backward_taps(padded, weight, planes, x_rows):
    stacked = y_shifts(padded)
    kernel = weight.reshape((3, 3, 3) + weight.shape[1:])
    summed = None
    for z_step in range(3):
        for x_step in range(3):
            product = jnp.einsum(
                "eoc,eozxy->czxy",
                kernel[z_step, x_step, ::-1],
                stacked[:, :, 2 - z_step : 2 - z_step + planes, 2 - x_step : 2 - x_step + x_rows],
                preferred_element_type=jnp.float32,
            )
            summed = product if summed is None else summed + product
    return summed


def weight_taps(grad, padded):
    planes, x_rows = (grad.shape[1], grad.shape[2])
    stacked = y_shifts(padded)
    result = []
    for z_step in range(3):
        for x_step in range(3):
            result.append(
                jnp.einsum(
                    "ozxy,eczxy->eoc",
                    grad,
                    stacked[:, :, z_step : z_step + planes, x_step : x_step + x_rows],
                    preferred_element_type=jnp.float32,
                )
            )
    return jnp.concatenate(result)


def frame_cols(tensor):
    return jnp.pad(tensor, ((0, 0), (0, 0), (0, 0), (1, 1)))


def channel_sums(tensor):
    return jnp.sum(tensor.astype(jnp.float32), axis=(1, 2, 3))


def butterfly_sum(flat, axes):
    for axis in axes:
        count = lax.axis_size(axis)
        if count & (count - 1):
            flat = lax.psum(flat, axis)
            continue
        bit = 1
        while bit < count:
            flat = flat + lax.ppermute(flat, axis, [(i, i ^ bit) for i in range(count)])
            bit *= 2
    return flat


def replicated_sum(flat, scatter_axis, other_axes):
    total = flat.shape[0]
    count = lax.axis_size(scatter_axis)
    chunks = jnp.pad(flat, (0, (-total) % count)).reshape(count, -1)
    owned = lax.all_to_all(chunks, scatter_axis, 0, 0, tiled=False).sum(0)
    owned = butterfly_sum(owned, other_axes)
    spread = lax.all_to_all(jnp.broadcast_to(owned, (count,) + owned.shape), scatter_axis, 0, 0, tiled=False)
    return spread.reshape(-1)[:total]


def per_device(latent, condition, cotangent, expand_kernel, mixing_matrix, project_kernel, offsets):
    planes, x_rows, y_cols = (latent.shape[1], latent.shape[2], latent.shape[3])
    hidden_width = mixing_matrix.shape[0]
    upper_half, lower_half = (latent[:CH], latent[CH:])
    cot_upper, cot_lower = (cotangent[:CH], cotangent[CH:])
    expand_offset = offsets[:hidden_width][:, None, None, None]
    mixing_offset = offsets[hidden_width : 2 * hidden_width][:, None, None, None]
    project_offset = offsets[2 * hidden_width :][:, None, None, None]
    inputs = jnp.concatenate([upper_half.astype(jnp.bfloat16), condition], axis=0)
    wide = frame_cols(extended(inputs, (("gz", 1), ("gx", 2)), 2))
    framed = wide[:, 1:-1, 1:-1]
    pre_wide = forward_taps(wide, expand_kernel, planes + 2, x_rows + 2) + expand_offset
    act_wide = jax.nn.silu(pre_wide).astype(jnp.bfloat16)
    pre_two_wide = (
        jnp.einsum("oc,czxy->ozxy", mixing_matrix, act_wide, preferred_element_type=jnp.float32)
        + mixing_offset
    )
    plane_at = lax.axis_index("gz") * planes - 1 + jnp.arange(planes + 2)
    row_at = lax.axis_index("gx") * x_rows - 1 + jnp.arange(x_rows + 2)
    inside = (
        ((plane_at >= 0) & (plane_at < planes * lax.axis_size("gz")))[:, None]
        & ((row_at >= 0) & (row_at < x_rows * lax.axis_size("gx")))[None, :]
    )
    act_two_wide = jnp.where(inside[None, :, :, None], jax.nn.silu(pre_two_wide), 0.0).astype(jnp.bfloat16)
    act_frame = frame_cols(act_two_wide)
    pre_one = pre_wide[:, 1:-1, 1:-1]
    act_one = act_wide[:, 1:-1, 1:-1]
    pre_two = pre_two_wide[:, 1:-1, 1:-1]
    scores = forward_taps(act_frame, project_kernel, planes, x_rows) + project_offset
    log_scale = jnp.tanh(scores[:CH])
    centered = lower_half - scores[CH:]
    recovered = centered * jnp.exp(-log_scale)
    score_grad = jnp.concatenate(
        [cot_lower * centered * (1.0 - log_scale * log_scale), cot_lower], axis=0
    ).astype(jnp.bfloat16)
    recovered, score_grad, lower_grad = (recovered, score_grad, cot_lower * jnp.exp(log_scale))
    score_frame = frame_cols(extended(score_grad, (("gz", 1), ("gx", 2)), 1))
    hidden_grad = backward_taps(score_frame, project_kernel, planes, x_rows)
    mix_grad = (hidden_grad * silu_slope(pre_two)).astype(jnp.bfloat16)
    back_one = jnp.einsum(
        "oc,ozxy->czxy", mixing_matrix, mix_grad, preferred_element_type=jnp.float32
    )
    first_grad = (back_one * silu_slope(pre_one)).astype(jnp.bfloat16)
    inner_first, inner_mix, inner_act = (first_grad, mix_grad, act_one)
    expand_term = weight_taps(inner_first, framed)
    mixing_term = jnp.einsum(
        "ozxy,czxy->oc", inner_mix, inner_act, preferred_element_type=jnp.float32
    )
    project_term = weight_taps(score_grad, act_frame)
    offset_term = jnp.concatenate(
        [channel_sums(inner_first), channel_sums(inner_mix), channel_sums(score_grad)]
    )
    terms = (expand_term, mixing_term, project_term, offset_term)
    flat = jnp.concatenate([t.reshape(-1) for t in terms])
    total = flat.shape[0]
    count = lax.axis_size("gz")
    chunks = jnp.pad(flat, (0, (-total) % count)).reshape(count, -1)
    owned = lax.all_to_all(chunks, "gz", 0, 0, tiled=False).sum(0)
    owned, first_grad = lax.optimization_barrier((owned, first_grad))
    factor = 1.0 / math.sqrt(float(planes * x_rows * y_cols))
    members = lax.axis_size("gx")
    owned = lax.all_to_all(
        jnp.broadcast_to(owned, (members,) + owned.shape), "gx", 0, 0, tiled=False
    ).sum(0) * factor
    first_frame = frame_cols(extended(first_grad, (("gz", 1), ("gx", 2)), 1))
    input_grad = backward_taps(first_frame, expand_kernel, planes, x_rows)
    spread = lax.all_to_all(jnp.broadcast_to(owned, (count,) + owned.shape), "gz", 0, 0, tiled=False)
    flat = spread.reshape(-1)[:total]
    pieces, start = [], 0
    for t in terms:
        pieces.append(flat[start : start + t.size].reshape(t.shape))
        start += t.size
    expand_sum, mixing_sum, project_sum, offset_sum = pieces
    restored = unsqueeze(jnp.concatenate([upper_half, recovered], axis=0))
    field_grad = unsqueeze(jnp.concatenate([cot_upper + input_grad[:CH], lower_grad], axis=0))
    condition_grad = input_grad[CH:]
    return (
        restored,
        field_grad,
        condition_grad,
        expand_sum,
        mixing_sum,
        project_sum,
        offset_sum,
    )


def solution(mesh):
    placed = (
        P(None, "gz", "gx", None),
        P(None, "gz", "gx", None),
        P(None, "gz", "gx", None),
        P(),
        P(),
        P(),
        P(),
    )
    return jax.shard_map(
        per_device,
        mesh=mesh,
        in_specs=placed,
        out_specs=(
            P("gz", "gx", None),
            P("gz", "gx", None),
            P(None, "gz", "gx", None),
            P(),
            P(),
            P(),
            P(),
        ),
        check_vma=False,
    )
```

```python
import math

import jax
import jax.numpy as jnp
import numpy as np
from jax import lax
from jax.sharding import PartitionSpec as P

CH = 4


def extended(cells, sides, width):
    for axis, dim in sides:
        count = lax.axis_size(axis)
        ends = count - 1
        head = lax.slice_in_dim(cells, 0, width, axis=dim)
        tail = lax.slice_in_dim(cells, cells.shape[dim] - width, cells.shape[dim], axis=dim)
        cells = jnp.concatenate(
            [
                lax.ppermute(tail, axis, [(i, (i + 1) % count) for i in range(ends)]),
                cells,
                lax.ppermute(head, axis, [((i + 1) % count, i) for i in range(ends)]),
            ],
            axis=dim,
        )
    return cells


def set_bits(value):
    parity_count = 0
    for bit_place in range(3):
        parity_count = parity_count + (value >> bit_place & 1)
    return parity_count


def haar_table():
    signs = np.zeros((8, 8), np.float32)
    for fine_index in range(8):
        for coef_index in range(8):
            parity = set_bits(fine_index & coef_index)
            signs[fine_index, coef_index] = (-1.0) ** parity / np.sqrt(8.0)
    return signs


def unsqueeze(coarse):
    haar_signs = jnp.asarray(haar_table())
    spread = jnp.einsum("pk,kzxy->pzxy", haar_signs, coarse, precision=lax.Precision.HIGHEST)
    planes, x_rows, y_cols = (coarse.shape[1], coarse.shape[2], coarse.shape[3])
    spread = spread.reshape(2, 2, 2, planes, x_rows, y_cols).transpose(3, 0, 4, 1, 5, 2)
    return spread.reshape(2 * planes, 2 * x_rows, 2 * y_cols)


def silu_slope(preact):
    sigma = jax.nn.sigmoid(preact)
    return sigma * (1.0 + preact * (1.0 - sigma))


def shift_stack(padded, x_rows):
    y_cols = padded.shape[3] - 2
    if padded.shape[0] > 16:
        steps = [(None, y_step) for y_step in range(3)]
    else:
        steps = [(x_step, y_step) for x_step in range(3) for y_step in range(3)]
    slices = []
    for x_step, y_step in steps:
        cut = padded[..., y_step : y_step + y_cols]
        if x_step is not None:
            cut = cut[:, :, x_step : x_step + x_rows]
        slices.append(cut)
    return jnp.stack(slices), len(steps) == 9


def forward_taps(padded, weight, planes, x_rows):
    stacked, full = shift_stack(padded, x_rows)
    kernel = weight.reshape((3, 3, 3) + weight.shape[1:])
    summed = None
    for z_step in range(3):
        for x_step in [None] if full else range(3):
            if full:
                taps = kernel[z_step].reshape((9,) + weight.shape[1:])
                window = stacked[:, :, z_step : z_step + planes]
            else:
                taps = kernel[z_step, x_step]
                window = stacked[:, :, z_step : z_step + planes, x_step : x_step + x_rows]
            product = jnp.einsum(
                "eoc,eczxy->ozxy", taps, window, preferred_element_type=jnp.float32
            )
            summed = product if summed is None else summed + product
    return summed


def backward_taps(padded, weight, planes, x_rows):
    stacked, full = shift_stack(padded, x_rows)
    kernel = weight.reshape((3, 3, 3) + weight.shape[1:])
    summed = None
    for z_step in range(3):
        for x_step in [None] if full else range(3):
            if full:
                taps = kernel[z_step, ::-1, ::-1].reshape((9,) + weight.shape[1:])
                window = stacked[:, :, 2 - z_step : 2 - z_step + planes]
            else:
                taps = kernel[z_step, x_step, ::-1]
                window = stacked[
                    :, :, 2 - z_step : 2 - z_step + planes, 2 - x_step : 2 - x_step + x_rows
                ]
            product = jnp.einsum(
                "eoc,eozxy->czxy", taps, window, preferred_element_type=jnp.float32
            )
            summed = product if summed is None else summed + product
    return summed


def weight_taps(grad, padded):
    planes, x_rows = (grad.shape[1], grad.shape[2])
    stacked, full = shift_stack(padded, x_rows)
    result = []
    for z_step in range(3):
        for x_step in [None] if full else range(3):
            if full:
                window = stacked[:, :, z_step : z_step + planes]
            else:
                window = stacked[:, :, z_step : z_step + planes, x_step : x_step + x_rows]
            result.append(
                jnp.einsum("ozxy,eczxy->eoc", grad, window, preferred_element_type=jnp.float32)
            )
    return jnp.concatenate(result)


def frame_cols(tensor):
    return jnp.pad(tensor, ((0, 0), (0, 0), (0, 0), (1, 1)))


def channel_sums(tensor):
    return jnp.sum(tensor.astype(jnp.float32), axis=(1, 2, 3))


def butterfly_sum(flat, axes):
    for axis in axes:
        count = lax.axis_size(axis)
        if count & (count - 1):
            flat = lax.psum(flat, axis)
            continue
        bit = 1
        while bit < count:
            flat = flat + lax.ppermute(flat, axis, [(i, i ^ bit) for i in range(count)])
            bit *= 2
    return flat


def replicated_sum(flat, scatter_axis, other_axes):
    total = flat.shape[0]
    count = lax.axis_size(scatter_axis)
    chunks = jnp.pad(flat, (0, (-total) % count)).reshape(count, -1)
    owned = lax.all_to_all(chunks, scatter_axis, 0, 0, tiled=False).sum(0)
    owned = butterfly_sum(owned, other_axes)
    spread = lax.all_to_all(jnp.broadcast_to(owned, (count,) + owned.shape), scatter_axis, 0, 0, tiled=False)
    return spread.reshape(-1)[:total]


def per_device(latent, condition, cotangent, expand_kernel, mixing_matrix, project_kernel, offsets):
    planes, x_rows, y_cols = (latent.shape[1], latent.shape[2], latent.shape[3])
    hidden_width = mixing_matrix.shape[0]
    upper_half, lower_half = (latent[:CH], latent[CH:])
    cot_upper, cot_lower = (cotangent[:CH], cotangent[CH:])
    expand_offset = offsets[:hidden_width][:, None, None, None]
    mixing_offset = offsets[hidden_width : 2 * hidden_width][:, None, None, None]
    project_offset = offsets[2 * hidden_width :][:, None, None, None]
    inputs = jnp.concatenate([upper_half.astype(jnp.bfloat16), condition], axis=0)
    wide = frame_cols(extended(inputs, (("gz", 1), ("gx", 2)), 2))
    framed = wide[:, 1:-1, 1:-1]
    pre_wide = forward_taps(wide, expand_kernel, planes + 2, x_rows + 2) + expand_offset
    act_wide = jax.nn.silu(pre_wide).astype(jnp.bfloat16)
    pre_two_wide = (
        jnp.einsum("oc,czxy->ozxy", mixing_matrix, act_wide, preferred_element_type=jnp.float32)
        + mixing_offset
    )
    plane_at = lax.axis_index("gz") * planes - 1 + jnp.arange(planes + 2)
    row_at = lax.axis_index("gx") * x_rows - 1 + jnp.arange(x_rows + 2)
    inside = (
        ((plane_at >= 0) & (plane_at < planes * lax.axis_size("gz")))[:, None]
        & ((row_at >= 0) & (row_at < x_rows * lax.axis_size("gx")))[None, :]
    )
    act_two_wide = jnp.where(inside[None, :, :, None], jax.nn.silu(pre_two_wide), 0.0).astype(jnp.bfloat16)
    act_frame = frame_cols(act_two_wide)
    pre_one = pre_wide[:, 1:-1, 1:-1]
    act_one = act_wide[:, 1:-1, 1:-1]
    pre_two = pre_two_wide[:, 1:-1, 1:-1]
    scores = forward_taps(act_frame, project_kernel, planes, x_rows) + project_offset
    log_scale = jnp.tanh(scores[:CH])
    centered = lower_half - scores[CH:]
    recovered = centered * jnp.exp(-log_scale)
    score_grad = jnp.concatenate(
        [cot_lower * centered * (1.0 - log_scale * log_scale), cot_lower], axis=0
    ).astype(jnp.bfloat16)
    recovered, score_grad, lower_grad = (recovered, score_grad, cot_lower * jnp.exp(log_scale))
    score_frame = frame_cols(extended(score_grad, (("gz", 1), ("gx", 2)), 1))
    hidden_grad = backward_taps(score_frame, project_kernel, planes, x_rows)
    mix_grad = (hidden_grad * silu_slope(pre_two)).astype(jnp.bfloat16)
    back_one = jnp.einsum(
        "oc,ozxy->czxy", mixing_matrix, mix_grad, preferred_element_type=jnp.float32
    )
    first_grad = (back_one * silu_slope(pre_one)).astype(jnp.bfloat16)
    inner_first, inner_mix, inner_act = (first_grad, mix_grad, act_one)
    expand_term = weight_taps(inner_first, framed)
    mixing_term = jnp.einsum(
        "ozxy,czxy->oc", inner_mix, inner_act, preferred_element_type=jnp.float32
    )
    project_term = weight_taps(score_grad, act_frame)
    offset_term = jnp.concatenate(
        [channel_sums(inner_first), channel_sums(inner_mix), channel_sums(score_grad)]
    )
    terms = (expand_term, mixing_term, project_term, offset_term)
    flat = jnp.concatenate([t.reshape(-1) for t in terms])
    total = flat.shape[0]
    count = lax.axis_size("gz")
    chunks = jnp.pad(flat, (0, (-total) % count)).reshape(count, -1)
    owned = lax.all_to_all(chunks, "gz", 0, 0, tiled=False).sum(0)
    owned, first_grad = lax.optimization_barrier((owned, first_grad))
    factor = 1.0 / math.sqrt(float(planes * x_rows * y_cols))
    owned = butterfly_sum(owned, ("gx",)) * factor
    first_frame = frame_cols(extended(first_grad, (("gz", 1), ("gx", 2)), 1))
    input_grad = backward_taps(first_frame, expand_kernel, planes, x_rows)
    spread = lax.all_to_all(jnp.broadcast_to(owned, (count,) + owned.shape), "gz", 0, 0, tiled=False)
    flat = spread.reshape(-1)[:total]
    pieces, start = [], 0
    for t in terms:
        pieces.append(flat[start : start + t.size].reshape(t.shape))
        start += t.size
    expand_sum, mixing_sum, project_sum, offset_sum = pieces
    restored = unsqueeze(jnp.concatenate([upper_half, recovered], axis=0))
    field_grad = unsqueeze(jnp.concatenate([cot_upper + input_grad[:CH], lower_grad], axis=0))
    condition_grad = input_grad[CH:]
    return (
        restored,
        field_grad,
        condition_grad,
        expand_sum,
        mixing_sum,
        project_sum,
        offset_sum,
    )


def solution(mesh):
    placed = (
        P(None, "gz", "gx", None),
        P(None, "gz", "gx", None),
        P(None, "gz", "gx", None),
        P(),
        P(),
        P(),
        P(),
    )
    return jax.shard_map(
        per_device,
        mesh=mesh,
        in_specs=placed,
        out_specs=(
            P("gz", "gx", None),
            P("gz", "gx", None),
            P(None, "gz", "gx", None),
            P(),
            P(),
            P(),
            P(),
        ),
        check_vma=False,
    )
```

```python
import math

import jax
import jax.numpy as jnp
import numpy as np
from jax import lax
from jax.sharding import PartitionSpec as P

CH = 4


def extended(cells, sides, width):
    for axis, dim in sides:
        count = lax.axis_size(axis)
        ends = count - 1
        head = lax.slice_in_dim(cells, 0, width, axis=dim)
        tail = lax.slice_in_dim(cells, cells.shape[dim] - width, cells.shape[dim], axis=dim)
        cells = jnp.concatenate(
            [
                lax.ppermute(tail, axis, [(i, (i + 1) % count) for i in range(ends)]),
                cells,
                lax.ppermute(head, axis, [((i + 1) % count, i) for i in range(ends)]),
            ],
            axis=dim,
        )
    return cells


def set_bits(value):
    parity_count = 0
    for bit_place in range(3):
        parity_count = parity_count + (value >> bit_place & 1)
    return parity_count


def haar_table():
    signs = np.zeros((8, 8), np.float32)
    for fine_index in range(8):
        for coef_index in range(8):
            parity = set_bits(fine_index & coef_index)
            signs[fine_index, coef_index] = (-1.0) ** parity / np.sqrt(8.0)
    return signs


def unsqueeze(coarse):
    haar_signs = jnp.asarray(haar_table())
    spread = jnp.einsum("pk,kzxy->pzxy", haar_signs, coarse, precision=lax.Precision.HIGHEST)
    planes, x_rows, y_cols = (coarse.shape[1], coarse.shape[2], coarse.shape[3])
    spread = spread.reshape(2, 2, 2, planes, x_rows, y_cols).transpose(3, 0, 4, 1, 5, 2)
    return spread.reshape(2 * planes, 2 * x_rows, 2 * y_cols)


def silu_slope(preact):
    sigma = jax.nn.sigmoid(preact)
    return sigma * (1.0 + preact * (1.0 - sigma))


def shift_stack(padded, x_rows):
    y_cols = padded.shape[3] - 2
    if padded.shape[0] > 64:
        steps = [(None, y_step) for y_step in range(3)]
    else:
        steps = [(x_step, y_step) for x_step in range(3) for y_step in range(3)]
    slices = []
    for x_step, y_step in steps:
        cut = padded[..., y_step : y_step + y_cols]
        if x_step is not None:
            cut = cut[:, :, x_step : x_step + x_rows]
        slices.append(cut)
    return jnp.stack(slices), len(steps) == 9


def forward_taps(padded, weight, planes, x_rows):
    stacked, full = shift_stack(padded, x_rows)
    kernel = weight.reshape((3, 3, 3) + weight.shape[1:])
    summed = None
    for z_step in range(3):
        for x_step in [None] if full else range(3):
            if full:
                taps = kernel[z_step].reshape((9,) + weight.shape[1:])
                window = stacked[:, :, z_step : z_step + planes]
            else:
                taps = kernel[z_step, x_step]
                window = stacked[:, :, z_step : z_step + planes, x_step : x_step + x_rows]
            product = jnp.einsum(
                "eoc,eczxy->ozxy", taps, window, preferred_element_type=jnp.float32
            )
            summed = product if summed is None else summed + product
    return summed


def backward_taps(padded, weight, planes, x_rows):
    stacked, full = shift_stack(padded, x_rows)
    kernel = weight.reshape((3, 3, 3) + weight.shape[1:])
    summed = None
    for z_step in range(3):
        for x_step in [None] if full else range(3):
            if full:
                taps = kernel[z_step, ::-1, ::-1].reshape((9,) + weight.shape[1:])
                window = stacked[:, :, 2 - z_step : 2 - z_step + planes]
            else:
                taps = kernel[z_step, x_step, ::-1]
                window = stacked[
                    :, :, 2 - z_step : 2 - z_step + planes, 2 - x_step : 2 - x_step + x_rows
                ]
            product = jnp.einsum(
                "eoc,eozxy->czxy", taps, window, preferred_element_type=jnp.float32
            )
            summed = product if summed is None else summed + product
    return summed


def weight_taps(grad, padded):
    planes, x_rows = (grad.shape[1], grad.shape[2])
    stacked, full = shift_stack(padded, x_rows)
    result = []
    for z_step in range(3):
        for x_step in [None] if full else range(3):
            if full:
                window = stacked[:, :, z_step : z_step + planes]
            else:
                window = stacked[:, :, z_step : z_step + planes, x_step : x_step + x_rows]
            result.append(
                jnp.einsum("ozxy,eczxy->eoc", grad, window, preferred_element_type=jnp.float32)
            )
    return jnp.concatenate(result)


def frame_cols(tensor):
    return jnp.pad(tensor, ((0, 0), (0, 0), (0, 0), (1, 1)))


def channel_sums(tensor):
    return jnp.sum(tensor.astype(jnp.float32), axis=(1, 2, 3))


def butterfly_sum(flat, axes):
    for axis in axes:
        count = lax.axis_size(axis)
        if count & (count - 1):
            flat = lax.psum(flat, axis)
            continue
        bit = 1
        while bit < count:
            flat = flat + lax.ppermute(flat, axis, [(i, i ^ bit) for i in range(count)])
            bit *= 2
    return flat


def replicated_sum(flat, scatter_axis, other_axes):
    total = flat.shape[0]
    count = lax.axis_size(scatter_axis)
    chunks = jnp.pad(flat, (0, (-total) % count)).reshape(count, -1)
    owned = lax.all_to_all(chunks, scatter_axis, 0, 0, tiled=False).sum(0)
    owned = butterfly_sum(owned, other_axes)
    spread = lax.all_to_all(jnp.broadcast_to(owned, (count,) + owned.shape), scatter_axis, 0, 0, tiled=False)
    return spread.reshape(-1)[:total]


def per_device(latent, condition, cotangent, expand_kernel, mixing_matrix, project_kernel, offsets):
    planes, x_rows, y_cols = (latent.shape[1], latent.shape[2], latent.shape[3])
    hidden_width = mixing_matrix.shape[0]
    upper_half, lower_half = (latent[:CH], latent[CH:])
    cot_upper, cot_lower = (cotangent[:CH], cotangent[CH:])
    expand_offset = offsets[:hidden_width][:, None, None, None]
    mixing_offset = offsets[hidden_width : 2 * hidden_width][:, None, None, None]
    project_offset = offsets[2 * hidden_width :][:, None, None, None]
    inputs = jnp.concatenate([upper_half.astype(jnp.bfloat16), condition], axis=0)
    wide = frame_cols(extended(inputs, (("gz", 1), ("gx", 2)), 2))
    framed = wide[:, 1:-1, 1:-1]
    pre_wide = forward_taps(wide, expand_kernel, planes + 2, x_rows + 2) + expand_offset
    act_wide = jax.nn.silu(pre_wide).astype(jnp.bfloat16)
    pre_two_wide = (
        jnp.einsum("oc,czxy->ozxy", mixing_matrix, act_wide, preferred_element_type=jnp.float32)
        + mixing_offset
    )
    plane_at = lax.axis_index("gz") * planes - 1 + jnp.arange(planes + 2)
    row_at = lax.axis_index("gx") * x_rows - 1 + jnp.arange(x_rows + 2)
    inside = (
        ((plane_at >= 0) & (plane_at < planes * lax.axis_size("gz")))[:, None]
        & ((row_at >= 0) & (row_at < x_rows * lax.axis_size("gx")))[None, :]
    )
    act_two_wide = jnp.where(inside[None, :, :, None], jax.nn.silu(pre_two_wide), 0.0).astype(jnp.bfloat16)
    act_frame = frame_cols(act_two_wide)
    pre_one = pre_wide[:, 1:-1, 1:-1]
    act_one = act_wide[:, 1:-1, 1:-1]
    pre_two = pre_two_wide[:, 1:-1, 1:-1]
    scores = forward_taps(act_frame, project_kernel, planes, x_rows) + project_offset
    log_scale = jnp.tanh(scores[:CH])
    centered = lower_half - scores[CH:]
    recovered = centered * jnp.exp(-log_scale)
    score_grad = jnp.concatenate(
        [cot_lower * centered * (1.0 - log_scale * log_scale), cot_lower], axis=0
    ).astype(jnp.bfloat16)
    recovered, score_grad, lower_grad = (recovered, score_grad, cot_lower * jnp.exp(log_scale))
    score_frame = frame_cols(extended(score_grad, (("gz", 1), ("gx", 2)), 1))
    hidden_grad = backward_taps(score_frame, project_kernel, planes, x_rows)
    mix_grad = (hidden_grad * silu_slope(pre_two)).astype(jnp.bfloat16)
    back_one = jnp.einsum(
        "oc,ozxy->czxy", mixing_matrix, mix_grad, preferred_element_type=jnp.float32
    )
    first_grad = (back_one * silu_slope(pre_one)).astype(jnp.bfloat16)
    inner_first, inner_mix, inner_act = (first_grad, mix_grad, act_one)
    expand_term = weight_taps(inner_first, framed)
    mixing_term = jnp.einsum(
        "ozxy,czxy->oc", inner_mix, inner_act, preferred_element_type=jnp.float32
    )
    project_term = weight_taps(score_grad, act_frame)
    offset_term = jnp.concatenate(
        [channel_sums(inner_first), channel_sums(inner_mix), channel_sums(score_grad)]
    )
    terms = (expand_term, mixing_term, project_term, offset_term)
    flat = jnp.concatenate([t.reshape(-1) for t in terms])
    total = flat.shape[0]
    count = lax.axis_size("gz")
    chunks = jnp.pad(flat, (0, (-total) % count)).reshape(count, -1)
    owned = lax.all_to_all(chunks, "gz", 0, 0, tiled=False).sum(0)
    owned, first_grad = lax.optimization_barrier((owned, first_grad))
    factor = 1.0 / math.sqrt(float(planes * x_rows * y_cols))
    owned = butterfly_sum(owned, ("gx",)) * factor
    first_frame = frame_cols(extended(first_grad, (("gz", 1), ("gx", 2)), 1))
    input_grad = backward_taps(first_frame, expand_kernel, planes, x_rows)
    spread = lax.all_to_all(jnp.broadcast_to(owned, (count,) + owned.shape), "gz", 0, 0, tiled=False)
    flat = spread.reshape(-1)[:total]
    pieces, start = [], 0
    for t in terms:
        pieces.append(flat[start : start + t.size].reshape(t.shape))
        start += t.size
    expand_sum, mixing_sum, project_sum, offset_sum = pieces
    restored = unsqueeze(jnp.concatenate([upper_half, recovered], axis=0))
    field_grad = unsqueeze(jnp.concatenate([cot_upper + input_grad[:CH], lower_grad], axis=0))
    condition_grad = input_grad[CH:]
    return (
        restored,
        field_grad,
        condition_grad,
        expand_sum,
        mixing_sum,
        project_sum,
        offset_sum,
    )


def solution(mesh):
    placed = (
        P(None, "gz", "gx", None),
        P(None, "gz", "gx", None),
        P(None, "gz", "gx", None),
        P(),
        P(),
        P(),
        P(),
    )
    return jax.shard_map(
        per_device,
        mesh=mesh,
        in_specs=placed,
        out_specs=(
            P("gz", "gx", None),
            P("gz", "gx", None),
            P(None, "gz", "gx", None),
            P(),
            P(),
            P(),
            P(),
        ),
        check_vma=False,
    )
```

```python
import math

import jax
import jax.numpy as jnp
import numpy as np
from jax import lax
from jax.sharding import PartitionSpec as P

CH = 4


def extended(cells, sides, width):
    for axis, dim in sides:
        count = lax.axis_size(axis)
        ends = count - 1
        head = lax.slice_in_dim(cells, 0, width, axis=dim)
        tail = lax.slice_in_dim(cells, cells.shape[dim] - width, cells.shape[dim], axis=dim)
        cells = jnp.concatenate(
            [
                lax.ppermute(tail, axis, [(i, (i + 1) % count) for i in range(ends)]),
                cells,
                lax.ppermute(head, axis, [((i + 1) % count, i) for i in range(ends)]),
            ],
            axis=dim,
        )
    return cells


def set_bits(value):
    parity_count = 0
    for bit_place in range(3):
        parity_count = parity_count + (value >> bit_place & 1)
    return parity_count


def haar_table():
    signs = np.zeros((8, 8), np.float32)
    for fine_index in range(8):
        for coef_index in range(8):
            parity = set_bits(fine_index & coef_index)
            signs[fine_index, coef_index] = (-1.0) ** parity / np.sqrt(8.0)
    return signs


def unsqueeze(coarse):
    haar_signs = jnp.asarray(haar_table())
    spread = jnp.einsum("pk,kzxy->pzxy", haar_signs, coarse, precision=lax.Precision.HIGHEST)
    planes, x_rows, y_cols = (coarse.shape[1], coarse.shape[2], coarse.shape[3])
    spread = spread.reshape(2, 2, 2, planes, x_rows, y_cols).transpose(3, 0, 4, 1, 5, 2)
    return spread.reshape(2 * planes, 2 * x_rows, 2 * y_cols)


def silu_slope(preact):
    sigma = jax.nn.sigmoid(preact)
    return sigma * (1.0 + preact * (1.0 - sigma))


def shift_stack(padded, x_rows):
    y_cols = padded.shape[3] - 2
    if padded.shape[0] > 16:
        steps = [(None, y_step) for y_step in range(3)]
    else:
        steps = [(x_step, y_step) for x_step in range(3) for y_step in range(3)]
    slices = []
    for x_step, y_step in steps:
        cut = padded[..., y_step : y_step + y_cols]
        if x_step is not None:
            cut = cut[:, :, x_step : x_step + x_rows]
        slices.append(cut)
    return jnp.stack(slices), len(steps) == 9


def forward_taps(padded, weight, planes, x_rows):
    stacked, full = shift_stack(padded, x_rows)
    kernel = weight.reshape((3, 3, 3) + weight.shape[1:])
    summed = None
    for z_step in range(3):
        for x_step in [None] if full else range(3):
            if full:
                taps = kernel[z_step].reshape((9,) + weight.shape[1:])
                window = stacked[:, :, z_step : z_step + planes]
            else:
                taps = kernel[z_step, x_step]
                window = stacked[:, :, z_step : z_step + planes, x_step : x_step + x_rows]
            product = jnp.einsum(
                "eoc,eczxy->ozxy", taps, window, preferred_element_type=jnp.float32
            )
            summed = product if summed is None else summed + product
    return summed


def backward_taps(padded, weight, planes, x_rows):
    stacked, full = shift_stack(padded, x_rows)
    kernel = weight.reshape((3, 3, 3) + weight.shape[1:])
    summed = None
    for z_step in range(3):
        for x_step in [None] if full else range(3):
            if full:
                taps = kernel[z_step, ::-1, ::-1].reshape((9,) + weight.shape[1:])
                window = stacked[:, :, 2 - z_step : 2 - z_step + planes]
            else:
                taps = kernel[z_step, x_step, ::-1]
                window = stacked[
                    :, :, 2 - z_step : 2 - z_step + planes, 2 - x_step : 2 - x_step + x_rows
                ]
            product = jnp.einsum(
                "eoc,eozxy->czxy", taps, window, preferred_element_type=jnp.float32
            )
            summed = product if summed is None else summed + product
    return summed


def weight_taps(grad, padded):
    planes, x_rows = (grad.shape[1], grad.shape[2])
    stacked, full = shift_stack(padded, x_rows)
    result = []
    for z_step in range(3):
        for x_step in [None] if full else range(3):
            if full:
                window = stacked[:, :, z_step : z_step + planes]
            else:
                window = stacked[:, :, z_step : z_step + planes, x_step : x_step + x_rows]
            result.append(
                jnp.einsum("ozxy,eczxy->eoc", grad, window, preferred_element_type=jnp.float32)
            )
    return jnp.concatenate(result)


def weight_taps_swapped(grad, padded):
    planes, x_rows = (padded.shape[1], padded.shape[2])
    spread = jnp.pad(grad, ((0, 0), (2, 2), (2, 2), (2, 2)))
    stacked, _ = shift_stack(spread, x_rows)
    result = []
    for z_step in range(3):
        window = stacked[:, :, 2 - z_step : 2 - z_step + planes]
        result.append(
            jnp.einsum("eozxy,czxy->eoc", window, padded, preferred_element_type=jnp.float32)[::-1]
        )
    return jnp.concatenate(result)


def frame_cols(tensor):
    return jnp.pad(tensor, ((0, 0), (0, 0), (0, 0), (1, 1)))


def channel_sums(tensor):
    return jnp.sum(tensor.astype(jnp.float32), axis=(1, 2, 3))


def butterfly_sum(flat, axes):
    for axis in axes:
        count = lax.axis_size(axis)
        if count & (count - 1):
            flat = lax.psum(flat, axis)
            continue
        bit = 1
        while bit < count:
            flat = flat + lax.ppermute(flat, axis, [(i, i ^ bit) for i in range(count)])
            bit *= 2
    return flat


def replicated_sum(flat, scatter_axis, other_axes):
    total = flat.shape[0]
    count = lax.axis_size(scatter_axis)
    chunks = jnp.pad(flat, (0, (-total) % count)).reshape(count, -1)
    owned = lax.all_to_all(chunks, scatter_axis, 0, 0, tiled=False).sum(0)
    owned = butterfly_sum(owned, other_axes)
    spread = lax.all_to_all(jnp.broadcast_to(owned, (count,) + owned.shape), scatter_axis, 0, 0, tiled=False)
    return spread.reshape(-1)[:total]


def per_device(latent, condition, cotangent, expand_kernel, mixing_matrix, project_kernel, offsets):
    planes, x_rows, y_cols = (latent.shape[1], latent.shape[2], latent.shape[3])
    hidden_width = mixing_matrix.shape[0]
    upper_half, lower_half = (latent[:CH], latent[CH:])
    cot_upper, cot_lower = (cotangent[:CH], cotangent[CH:])
    expand_offset = offsets[:hidden_width][:, None, None, None]
    mixing_offset = offsets[hidden_width : 2 * hidden_width][:, None, None, None]
    project_offset = offsets[2 * hidden_width :][:, None, None, None]
    inputs = jnp.concatenate([upper_half.astype(jnp.bfloat16), condition], axis=0)
    wide = frame_cols(extended(inputs, (("gz", 1), ("gx", 2)), 2))
    framed = wide[:, 1:-1, 1:-1]
    pre_wide = forward_taps(wide, expand_kernel, planes + 2, x_rows + 2) + expand_offset
    act_wide = jax.nn.silu(pre_wide).astype(jnp.bfloat16)
    pre_two_wide = (
        jnp.einsum("oc,czxy->ozxy", mixing_matrix, act_wide, preferred_element_type=jnp.float32)
        + mixing_offset
    )
    plane_at = lax.axis_index("gz") * planes - 1 + jnp.arange(planes + 2)
    row_at = lax.axis_index("gx") * x_rows - 1 + jnp.arange(x_rows + 2)
    inside = (
        ((plane_at >= 0) & (plane_at < planes * lax.axis_size("gz")))[:, None]
        & ((row_at >= 0) & (row_at < x_rows * lax.axis_size("gx")))[None, :]
    )
    act_two_wide = jnp.where(inside[None, :, :, None], jax.nn.silu(pre_two_wide), 0.0).astype(jnp.bfloat16)
    act_frame = frame_cols(act_two_wide)
    pre_one = pre_wide[:, 1:-1, 1:-1]
    act_one = act_wide[:, 1:-1, 1:-1]
    pre_two = pre_two_wide[:, 1:-1, 1:-1]
    scores = forward_taps(act_frame, project_kernel, planes, x_rows) + project_offset
    log_scale = jnp.tanh(scores[:CH])
    centered = lower_half - scores[CH:]
    recovered = centered * jnp.exp(-log_scale)
    score_grad = jnp.concatenate(
        [cot_lower * centered * (1.0 - log_scale * log_scale), cot_lower], axis=0
    ).astype(jnp.bfloat16)
    recovered, score_grad, lower_grad = (recovered, score_grad, cot_lower * jnp.exp(log_scale))
    score_frame = frame_cols(extended(score_grad, (("gz", 1), ("gx", 2)), 1))
    hidden_grad = backward_taps(score_frame, project_kernel, planes, x_rows)
    mix_grad = (hidden_grad * silu_slope(pre_two)).astype(jnp.bfloat16)
    back_one = jnp.einsum(
        "oc,ozxy->czxy", mixing_matrix, mix_grad, preferred_element_type=jnp.float32
    )
    first_grad = (back_one * silu_slope(pre_one)).astype(jnp.bfloat16)
    inner_first, inner_mix, inner_act = (first_grad, mix_grad, act_one)
    expand_term = weight_taps(inner_first, framed)
    mixing_term = jnp.einsum(
        "ozxy,czxy->oc", inner_mix, inner_act, preferred_element_type=jnp.float32
    )
    project_term = weight_taps_swapped(score_grad, act_frame)
    offset_term = jnp.concatenate(
        [channel_sums(inner_first), channel_sums(inner_mix), channel_sums(score_grad)]
    )
    terms = (expand_term, mixing_term, project_term, offset_term)
    flat = jnp.concatenate([t.reshape(-1) for t in terms])
    total = flat.shape[0]
    count = lax.axis_size("gz")
    chunks = jnp.pad(flat, (0, (-total) % count)).reshape(count, -1)
    owned = lax.all_to_all(chunks, "gz", 0, 0, tiled=False).sum(0)
    owned, first_grad = lax.optimization_barrier((owned, first_grad))
    factor = 1.0 / math.sqrt(float(planes * x_rows * y_cols))
    owned = butterfly_sum(owned, ("gx",)) * factor
    first_frame = frame_cols(extended(first_grad, (("gz", 1), ("gx", 2)), 1))
    input_grad = backward_taps(first_frame, expand_kernel, planes, x_rows)
    spread = lax.all_to_all(jnp.broadcast_to(owned, (count,) + owned.shape), "gz", 0, 0, tiled=False)
    flat = spread.reshape(-1)[:total]
    pieces, start = [], 0
    for t in terms:
        pieces.append(flat[start : start + t.size].reshape(t.shape))
        start += t.size
    expand_sum, mixing_sum, project_sum, offset_sum = pieces
    restored = unsqueeze(jnp.concatenate([upper_half, recovered], axis=0))
    field_grad = unsqueeze(jnp.concatenate([cot_upper + input_grad[:CH], lower_grad], axis=0))
    condition_grad = input_grad[CH:]
    return (
        restored,
        field_grad,
        condition_grad,
        expand_sum,
        mixing_sum,
        project_sum,
        offset_sum,
    )


def solution(mesh):
    placed = (
        P(None, "gz", "gx", None),
        P(None, "gz", "gx", None),
        P(None, "gz", "gx", None),
        P(),
        P(),
        P(),
        P(),
    )
    return jax.shard_map(
        per_device,
        mesh=mesh,
        in_specs=placed,
        out_specs=(
            P("gz", "gx", None),
            P("gz", "gx", None),
            P(None, "gz", "gx", None),
            P(),
            P(),
            P(),
            P(),
        ),
        check_vma=False,
    )
```

```python
import math

import jax
import jax.numpy as jnp
import numpy as np
from jax import lax
from jax.sharding import PartitionSpec as P

CH = 4


def extended(cells, sides, width):
    for axis, dim in sides:
        count = lax.axis_size(axis)
        ends = count - 1
        head = lax.slice_in_dim(cells, 0, width, axis=dim)
        tail = lax.slice_in_dim(cells, cells.shape[dim] - width, cells.shape[dim], axis=dim)
        cells = jnp.concatenate(
            [
                lax.ppermute(tail, axis, [(i, (i + 1) % count) for i in range(ends)]),
                cells,
                lax.ppermute(head, axis, [((i + 1) % count, i) for i in range(ends)]),
            ],
            axis=dim,
        )
    return cells


def set_bits(value):
    parity_count = 0
    for bit_place in range(3):
        parity_count = parity_count + (value >> bit_place & 1)
    return parity_count


def haar_table():
    signs = np.zeros((8, 8), np.float32)
    for fine_index in range(8):
        for coef_index in range(8):
            parity = set_bits(fine_index & coef_index)
            signs[fine_index, coef_index] = (-1.0) ** parity / np.sqrt(8.0)
    return signs


def unsqueeze(coarse):
    haar_signs = jnp.asarray(haar_table())
    spread = jnp.einsum("pk,kzxy->pzxy", haar_signs, coarse, precision=lax.Precision.HIGHEST)
    planes, x_rows, y_cols = (coarse.shape[1], coarse.shape[2], coarse.shape[3])
    spread = spread.reshape(2, 2, 2, planes, x_rows, y_cols).transpose(3, 0, 4, 1, 5, 2)
    return spread.reshape(2 * planes, 2 * x_rows, 2 * y_cols)


def silu_slope(preact):
    sigma = jax.nn.sigmoid(preact)
    return sigma * (1.0 + preact * (1.0 - sigma))


def shift_stack(padded, x_rows):
    y_cols = padded.shape[3] - 2
    if padded.shape[0] > 16:
        steps = [(None, y_step) for y_step in range(3)]
    else:
        steps = [(x_step, y_step) for x_step in range(3) for y_step in range(3)]
    slices = []
    for x_step, y_step in steps:
        cut = padded[..., y_step : y_step + y_cols]
        if x_step is not None:
            cut = cut[:, :, x_step : x_step + x_rows]
        slices.append(cut)
    return jnp.stack(slices), len(steps) == 9


def forward_taps(padded, weight, planes, x_rows):
    stacked, full = shift_stack(padded, x_rows)
    kernel = weight.reshape((3, 3, 3) + weight.shape[1:])
    summed = None
    for z_step in range(3):
        for x_step in [None] if full else range(3):
            if full:
                taps = kernel[z_step].reshape((9,) + weight.shape[1:])
                window = stacked[:, :, z_step : z_step + planes]
            else:
                taps = kernel[z_step, x_step]
                window = stacked[:, :, z_step : z_step + planes, x_step : x_step + x_rows]
            product = jnp.einsum(
                "eoc,eczxy->ozxy", taps, window, preferred_element_type=jnp.float32
            )
            summed = product if summed is None else summed + product
    return summed


def backward_taps(padded, weight, planes, x_rows):
    stacked, full = shift_stack(padded, x_rows)
    kernel = weight.reshape((3, 3, 3) + weight.shape[1:])
    summed = None
    for z_step in range(3):
        for x_step in [None] if full else range(3):
            if full:
                taps = kernel[z_step, ::-1, ::-1].reshape((9,) + weight.shape[1:])
                window = stacked[:, :, 2 - z_step : 2 - z_step + planes]
            else:
                taps = kernel[z_step, x_step, ::-1]
                window = stacked[
                    :, :, 2 - z_step : 2 - z_step + planes, 2 - x_step : 2 - x_step + x_rows
                ]
            product = jnp.einsum(
                "eoc,eozxy->czxy", taps, window, preferred_element_type=jnp.float32
            )
            summed = product if summed is None else summed + product
    return summed


def weight_taps(grad, padded):
    planes, x_rows = (grad.shape[1], grad.shape[2])
    stacked, full = shift_stack(padded, x_rows)
    result = []
    for z_step in range(3):
        for x_step in [None] if full else range(3):
            if full:
                window = stacked[:, :, z_step : z_step + planes]
            else:
                window = stacked[:, :, z_step : z_step + planes, x_step : x_step + x_rows]
            result.append(
                jnp.einsum("ozxy,eczxy->eoc", grad, window, preferred_element_type=jnp.float32)
            )
    return jnp.concatenate(result)


def frame_cols(tensor):
    return jnp.pad(tensor, ((0, 0), (0, 0), (0, 0), (1, 1)))


def channel_sums(tensor):
    return jnp.sum(tensor.astype(jnp.float32), axis=(1, 2, 3))


def butterfly_sum(flat, axes):
    for axis in axes:
        count = lax.axis_size(axis)
        if count & (count - 1):
            flat = lax.psum(flat, axis)
            continue
        bit = count // 2
        while bit >= 1:
            flat = flat + lax.ppermute(flat, axis, [(i, i ^ bit) for i in range(count)])
            bit //= 2
    return flat


def replicated_sum(flat, scatter_axis, other_axes):
    total = flat.shape[0]
    count = lax.axis_size(scatter_axis)
    chunks = jnp.pad(flat, (0, (-total) % count)).reshape(count, -1)
    owned = lax.all_to_all(chunks, scatter_axis, 0, 0, tiled=False).sum(0)
    owned = butterfly_sum(owned, other_axes)
    spread = lax.all_to_all(jnp.broadcast_to(owned, (count,) + owned.shape), scatter_axis, 0, 0, tiled=False)
    return spread.reshape(-1)[:total]


def per_device(latent, condition, cotangent, expand_kernel, mixing_matrix, project_kernel, offsets):
    planes, x_rows, y_cols = (latent.shape[1], latent.shape[2], latent.shape[3])
    hidden_width = mixing_matrix.shape[0]
    upper_half, lower_half = (latent[:CH], latent[CH:])
    cot_upper, cot_lower = (cotangent[:CH], cotangent[CH:])
    expand_offset = offsets[:hidden_width][:, None, None, None]
    mixing_offset = offsets[hidden_width : 2 * hidden_width][:, None, None, None]
    project_offset = offsets[2 * hidden_width :][:, None, None, None]
    inputs = jnp.concatenate([upper_half.astype(jnp.bfloat16), condition], axis=0)
    wide = frame_cols(extended(inputs, (("gz", 1), ("gx", 2)), 2))
    framed = wide[:, 1:-1, 1:-1]
    pre_wide = forward_taps(wide, expand_kernel, planes + 2, x_rows + 2) + expand_offset
    act_wide = jax.nn.silu(pre_wide).astype(jnp.bfloat16)
    pre_two_wide = (
        jnp.einsum("oc,czxy->ozxy", mixing_matrix, act_wide, preferred_element_type=jnp.float32)
        + mixing_offset
    )
    plane_at = lax.axis_index("gz") * planes - 1 + jnp.arange(planes + 2)
    row_at = lax.axis_index("gx") * x_rows - 1 + jnp.arange(x_rows + 2)
    inside = (
        ((plane_at >= 0) & (plane_at < planes * lax.axis_size("gz")))[:, None]
        & ((row_at >= 0) & (row_at < x_rows * lax.axis_size("gx")))[None, :]
    )
    act_two_wide = jnp.where(inside[None, :, :, None], jax.nn.silu(pre_two_wide), 0.0).astype(jnp.bfloat16)
    act_frame = frame_cols(act_two_wide)
    pre_one = pre_wide[:, 1:-1, 1:-1]
    act_one = act_wide[:, 1:-1, 1:-1]
    pre_two = pre_two_wide[:, 1:-1, 1:-1]
    scores = forward_taps(act_frame, project_kernel, planes, x_rows) + project_offset
    log_scale = jnp.tanh(scores[:CH])
    centered = lower_half - scores[CH:]
    recovered = centered * jnp.exp(-log_scale)
    score_grad = jnp.concatenate(
        [cot_lower * centered * (1.0 - log_scale * log_scale), cot_lower], axis=0
    ).astype(jnp.bfloat16)
    recovered, score_grad, lower_grad = (recovered, score_grad, cot_lower * jnp.exp(log_scale))
    score_frame = frame_cols(extended(score_grad, (("gz", 1), ("gx", 2)), 1))
    hidden_grad = backward_taps(score_frame, project_kernel, planes, x_rows)
    mix_grad = (hidden_grad * silu_slope(pre_two)).astype(jnp.bfloat16)
    back_one = jnp.einsum(
        "oc,ozxy->czxy", mixing_matrix, mix_grad, preferred_element_type=jnp.float32
    )
    first_grad = (back_one * silu_slope(pre_one)).astype(jnp.bfloat16)
    inner_first, inner_mix, inner_act = (first_grad, mix_grad, act_one)
    expand_term = weight_taps(inner_first, framed)
    mixing_term = jnp.einsum(
        "ozxy,czxy->oc", inner_mix, inner_act, preferred_element_type=jnp.float32
    )
    project_term = weight_taps(score_grad, act_frame)
    offset_term = jnp.concatenate(
        [channel_sums(inner_first), channel_sums(inner_mix), channel_sums(score_grad)]
    )
    terms = (expand_term, mixing_term, project_term, offset_term)
    flat = jnp.concatenate([t.reshape(-1) for t in terms])
    total = flat.shape[0]
    count = lax.axis_size("gz")
    chunks = jnp.pad(flat, (0, (-total) % count)).reshape(count, -1)
    owned = lax.all_to_all(chunks, "gz", 0, 0, tiled=False).sum(0)
    owned, first_grad = lax.optimization_barrier((owned, first_grad))
    factor = 1.0 / math.sqrt(float(planes * x_rows * y_cols))
    owned = butterfly_sum(owned, ("gx",)) * factor
    first_frame = frame_cols(extended(first_grad, (("gz", 1), ("gx", 2)), 1))
    input_grad = backward_taps(first_frame, expand_kernel, planes, x_rows)
    spread = lax.all_to_all(jnp.broadcast_to(owned, (count,) + owned.shape), "gz", 0, 0, tiled=False)
    flat = spread.reshape(-1)[:total]
    pieces, start = [], 0
    for t in terms:
        pieces.append(flat[start : start + t.size].reshape(t.shape))
        start += t.size
    expand_sum, mixing_sum, project_sum, offset_sum = pieces
    restored = unsqueeze(jnp.concatenate([upper_half, recovered], axis=0))
    field_grad = unsqueeze(jnp.concatenate([cot_upper + input_grad[:CH], lower_grad], axis=0))
    condition_grad = input_grad[CH:]
    return (
        restored,
        field_grad,
        condition_grad,
        expand_sum,
        mixing_sum,
        project_sum,
        offset_sum,
    )


def solution(mesh):
    placed = (
        P(None, "gz", "gx", None),
        P(None, "gz", "gx", None),
        P(None, "gz", "gx", None),
        P(),
        P(),
        P(),
        P(),
    )
    return jax.shard_map(
        per_device,
        mesh=mesh,
        in_specs=placed,
        out_specs=(
            P("gz", "gx", None),
            P("gz", "gx", None),
            P(None, "gz", "gx", None),
            P(),
            P(),
            P(),
            P(),
        ),
        check_vma=False,
    )
```
